128 devices in a mesh: seq: 16 (over z_lo, y, core), head: 8 (over z_hi, x).
Axes of the slice: x: 4, y: 4, z: 4 (z_hi: 2, z_lo: 2; z = z_hi * 2 + z_lo), core: 2. Of those that a mesh axis runs over, the one named last changes fastest.
Arguments:
- inputs: bfloat16 [16384, 5376], P(('seq', 'head')), may hold values from -18 to 18
- queries: bfloat16 [16384, 4096], P('seq', 'head'), may hold values from -12 to 12
- key_rows: bfloat16 [16384, 2048], P('seq', 'head'), may hold values from -12 to 12
- values: bfloat16 [16384, 2048], P('seq', 'head'), may hold values from -6 to 6
- out_grad: bfloat16 [16384, 4096], P('seq', 'head'), may hold values from -6 to 6
- band_start: int32 [16384], P('seq'), may hold values from 0 to 16383, as said below
- owners: int32 [8, 6], replicated, may hold values from 0 to 15, as said below
Outputs:
- left_stat: float32 [16, 8, 1024, 1024], P('seq', 'head')
- right_stat: float32 [16, 8, 1024, 1024], P('seq', 'head')
The draws below stay inside these ranges and needn't reach their ends.
Inputs may be any that keep to these rules, and one draw needn't show every extreme that they name: band_start[i] lies between i - 1023 and i, and never decreases with i. `owners`: the 6 entries of a row differ.
All inputs are finite; a program needn't handle non-finite values.
Results may differ from the reference program's by a relative error of at most 0.015.
Values may be sent and summed in bfloat16 or wider, within the bound.
No kernel may reach another device: no remote copies, remote signals or barrier semaphores. Data moves between devices by JAX's collectives and lax.ppermute only.
A program may use at most 128 MiB of HBM per device.

```python
import jax
import jax.numpy as jnp
from jax import lax

D = 5376
HD = 128
KV_DEV = 2
QPK = 2
WINDOW = 1024
BLOCK = 1024
TOK_DEV = 1024
TOKENS = 16384
KVH = 16
QH = 32
CPD = 1024
NBLK = 6
N_SEQ = 16
N_HEAD = 8


def drawn_parts(key):
    base_keys = jnp.clip(jax.random.normal(jax.random.fold_in(key, 11), (TOKENS, KVH, HD), jnp.float32), -6.0, 6.0)
    base_queries = jnp.clip(jax.random.normal(jax.random.fold_in(key, 12), (TOKENS, KVH, QPK, HD), jnp.float32), -6.0, 6.0)
    base_queries = jnp.clip(base_queries, -12.0, 12.0).reshape(TOKENS, QH * HD)
    base_keys = jnp.clip(base_keys, -12.0, 12.0).reshape(TOKENS, KVH * HD)
    return (base_queries, base_keys)


def draw_queries(key, part):
    return drawn_parts(key)[0].astype(jnp.bfloat16)


def draw_key_rows(key, part):
    return drawn_parts(key)[1].astype(jnp.bfloat16)


def draw_inputs(key, part):
    position_scale = 1.0 + 2.0 * jnp.arange(TOKENS, dtype=jnp.float32) / (TOKENS - 1)
    base_rows = jnp.clip(jax.random.normal(jax.random.fold_in(key, 22), (TOKENS, D), jnp.float32), -6.0, 6.0)
    return (base_rows * position_scale[:, None]).astype(jnp.bfloat16)


def draw_band_start(key, part):
    index_rows = jnp.arange(TOKENS, dtype=jnp.int32)
    coin_marks = jax.random.randint(key, (TOKENS,), 0, 4 * WINDOW)
    starts = (coin_marks == 0) | (index_rows == 0) | (index_rows == TOKENS - 1)
    doc_first = lax.cummax(jnp.where(starts, index_rows, 0), axis=0)
    return jnp.maximum(index_rows - WINDOW + 1, doc_first).astype(jnp.int32)


def draw_owners(key, part):

    def one_row(current_row_index):
        token_permutation_order = jax.random.permutation(jax.random.fold_in(key, current_row_index), N_SEQ).astype(jnp.int32)
        slot_ids = jnp.arange(N_SEQ, dtype=jnp.int32)
        document_end_flags = (slot_ids == 0) | (slot_ids == N_SEQ - 1)
        extra_score_bias = jnp.where((current_row_index == 0) & document_end_flags, N_SEQ, 0).astype(jnp.int32)
        attention_logits = token_permutation_order + extra_score_bias
        chosen = lax.top_k(attention_logits, NBLK)[1]
        return chosen.astype(jnp.int32)
    return jax.vmap(one_row)(jnp.arange(N_HEAD, dtype=jnp.int32))


def block_scale(own_key, dims, shards, low, high):
    def one(axis_at, shards_of):
        draws = jax.random.uniform(jax.random.fold_in(jax.random.fold_in(own_key, 6), axis_at), (shards_of,), jnp.float32, low / len(shards), high / len(shards))
        return jnp.repeat(jnp.exp(draws), dims[axis_at] // shards_of).reshape((-1,) + (1,) * (len(dims) - axis_at - 1))

    level = one(*shards[0])
    for cut in shards[1:]:
        level = level * one(*cut)
    return level


def gaussian(own_key, shape, scale, reach, shards=(), held_as=jnp.bfloat16):
    array = jax.random.normal(own_key, shape, jnp.float32) * scale
    if len(shards) > 0:
        array = block_scale(own_key, shape, shards, -0.22, 0.18) * array
    return jnp.clip(array, min=-reach, max=reach).astype(held_as)


def setup_inputs(seed: int = 0) -> dict:
    keys = jax.random.split(jax.random.key(seed), 8)
    return {
        "inputs": draw_inputs(jax.random.fold_in(keys[7], 71), 0),
        "queries": draw_queries(jax.random.fold_in(keys[7], 71), 0),
        "key_rows": draw_key_rows(jax.random.fold_in(keys[7], 71), 0),
        "values": gaussian(keys[3], (TOKENS, KVH * HD), 1.0, 6.0, ((0, 16), (1, 8))),
        "out_grad": gaussian(keys[4], (TOKENS, QH * HD), 1.0, 6.0, ((0, 16), (1, 8))),
        "band_start": draw_band_start(jax.random.fold_in(keys[7], 71), 0),
        "owners": draw_owners(jax.random.fold_in(keys[7], 71), 0),
    }


score_scale = 168.0 ** -0.5
rotary_frequency_base = 10000.0
neg_large = -1e30
top_precision = lax.Precision.HIGHEST


def rope_tables(positions, head_size):
    half_size = head_size // 2
    frequency = jnp.power(rotary_frequency_base, -2.0 * jnp.arange(half_size, dtype=jnp.float32) / head_size)
    angles = positions.astype(jnp.float32)[:, None] * frequency[None, :]
    cosine_table = jnp.concatenate([jnp.cos(angles), jnp.cos(angles)], 1)
    sine_table = jnp.concatenate([jnp.sin(angles), jnp.sin(angles)], 1)
    return cosine_table, sine_table


def unrotate(gradient, cosine_table, sine_table):
    half_size = gradient.shape[-1] // 2
    scaled = gradient * sine_table
    turned = jnp.concatenate([-scaled[..., half_size:], scaled[..., :half_size]], -1)
    return gradient * cosine_table - turned


def low_copy(tensor):
    rounded = lax.optimization_barrier(tensor.astype(jnp.bfloat16))
    return rounded.astype(jnp.float32)


def reference(inputs, queries, key_rows, values, out_grad, band_start, owners):
    block_rows = min(512, TOKENS)
    span_rows = block_rows + WINDOW
    query_heads = queries.astype(jnp.float32).reshape(TOKENS, KVH, QPK, HD)
    out_heads = out_grad.astype(jnp.float32).reshape(TOKENS, KVH, QPK, HD)
    front_zero = jnp.zeros((WINDOW, KVH, HD), jnp.float32)
    gathered_key_rows = jnp.concatenate([front_zero, key_rows.astype(jnp.float32).reshape(TOKENS, KVH, HD)], 0)
    value_all = jnp.concatenate([front_zero, values.astype(jnp.float32).reshape(TOKENS, KVH, HD)], 0)

    def one_block(totals, offset):
        grad_keys, grad_values = totals
        query_part = lax.dynamic_slice_in_dim(query_heads, offset, block_rows, 0)
        out_part = lax.dynamic_slice_in_dim(out_heads, offset, block_rows, 0)
        key_part = lax.dynamic_slice_in_dim(gathered_key_rows, offset, span_rows, 0)
        value_part = lax.dynamic_slice_in_dim(value_all, offset, span_rows, 0)
        band_part = lax.dynamic_slice_in_dim(band_start, offset, block_rows, 0)
        query_pos = offset + jnp.arange(block_rows, dtype=jnp.int32)
        key_pos = offset - WINDOW + jnp.arange(span_rows, dtype=jnp.int32)
        allowed = (key_pos[None, :] >= band_part[:, None]) & (key_pos[None, :] <= query_pos[:, None])
        attention_logits = jnp.einsum("qgrh,kgh->grqk", query_part, key_part, precision=top_precision) * score_scale
        masked = jnp.where(allowed, attention_logits, neg_large)
        row_top = jnp.max(masked, -1, keepdims=True)
        exponent = jnp.where(allowed, jnp.exp(masked - row_top), 0.0)
        attend = exponent / jnp.sum(exponent, -1, keepdims=True)
        attend_low = low_copy(attend)
        grad_attend = jnp.einsum("qgrh,kgh->grqk", out_part, value_part, precision=top_precision)
        row_dot = jnp.sum(attend * grad_attend, -1, keepdims=True)
        grad_score = low_copy(attend * (grad_attend - row_dot) * score_scale)
        query_term = jnp.einsum("grqk,kgh->qgrh", grad_score, key_part, precision=top_precision)
        key_term = jnp.einsum("grqk,qgrh->kgh", grad_score, query_part, precision=top_precision)
        value_term = jnp.einsum("grqk,qgrh->kgh", attend_low, out_part, precision=top_precision)
        grad_keys = lax.dynamic_update_slice_in_dim(
            grad_keys, lax.dynamic_slice_in_dim(grad_keys, offset, span_rows, 0) + key_term, offset, 0)
        grad_values = lax.dynamic_update_slice_in_dim(
            grad_values, lax.dynamic_slice_in_dim(grad_values, offset, span_rows, 0) + value_term, offset, 0)
        return (grad_keys, grad_values), query_term

    offsets = jnp.arange(TOKENS // block_rows, dtype=jnp.int32) * block_rows
    start_pair = (jnp.zeros((TOKENS + WINDOW, KVH, HD), jnp.float32),
                  jnp.zeros((TOKENS + WINDOW, KVH, HD), jnp.float32))
    (grad_keys, grad_values), query_blocks = lax.scan(one_block, start_pair, offsets)
    grad_query = query_blocks.reshape(TOKENS, KVH * QPK, HD)
    grad_keys = grad_keys[WINDOW:]
    grad_values = grad_values[WINDOW:]
    cosine_table, sine_table = rope_tables(jnp.arange(TOKENS, dtype=jnp.int32), HD)
    query_pre = unrotate(grad_query, cosine_table[:, None, :], sine_table[:, None, :])
    key_pre = unrotate(grad_keys, cosine_table[:, None, :], sine_table[:, None, :])
    column_grads = jnp.concatenate([
        query_pre.reshape(TOKENS, N_HEAD, KV_DEV * QPK * HD),
        key_pre.reshape(TOKENS, N_HEAD, KV_DEV * HD),
        grad_values.reshape(TOKENS, N_HEAD, KV_DEV * HD)], 2).reshape(TOKENS, N_HEAD * CPD).astype(jnp.bfloat16)

    shard_inputs = inputs.reshape(N_SEQ, TOK_DEV, D)
    shard_grads = column_grads.reshape(N_SEQ, TOK_DEV, N_HEAD * CPD)

    def add_shard(total, shard_pair):
        term = jnp.dot(shard_pair[0].T, shard_pair[1], preferred_element_type=jnp.float32)
        return total + low_copy(term), None

    summed, unused = lax.scan(add_shard, jnp.zeros((D, N_HEAD * CPD), jnp.float32), (shard_inputs, shard_grads))
    gradient = summed.astype(jnp.bfloat16)
    padded = jnp.pad(gradient, ((0, NBLK * BLOCK - D), (0, 0)))
    left_stat = jnp.zeros((N_SEQ, N_HEAD, BLOCK, BLOCK), jnp.float32)
    right_stat = jnp.zeros((N_SEQ, N_HEAD, CPD, CPD), jnp.float32)
    for group_index in range(N_HEAD):
        for block_index in range(NBLK):
            part_rows = padded[block_index * BLOCK:(block_index + 1) * BLOCK, group_index * CPD:(group_index + 1) * CPD]
            holder = owners[group_index, block_index]
            left_value = jnp.dot(part_rows, part_rows.T, preferred_element_type=jnp.float32) / TOKENS
            right_value = jnp.dot(part_rows.T, part_rows, preferred_element_type=jnp.float32) / TOKENS
            left_stat = left_stat.at[holder, group_index].set(left_value)
            right_stat = right_stat.at[holder, group_index].set(right_value)
    return (left_stat, right_stat)
```

```python
import jax
import jax.numpy as jnp
from jax import lax
from jax.sharding import PartitionSpec as P

D = 5376
HD = 128
KV_DEV = 2
QPK = 2
WINDOW = 1024
BLOCK = 1024
NBLK = 6


score_scale = 168.0 ** (-0.5)
rotary_frequency_base = 10000.0
neg_large = -1e30


def shifted(value, axis, steps):
    count = lax.axis_size(axis)
    initial, last = (max(0, -steps), min(count, count - steps))
    return lax.ppermute(value, axis, [(source, source + steps) for source in range(initial, last)])


def rope_tables(positions, head_size):
    half_size = head_size // 2
    frequency = jnp.power(
        rotary_frequency_base, -2.0 * jnp.arange(half_size, dtype=jnp.float32) / head_size
    )
    angles = positions.astype(jnp.float32)[:, None] * frequency[None, :]
    cosine_table = jnp.concatenate([jnp.cos(angles), jnp.cos(angles)], 1)
    sine_table = jnp.concatenate([jnp.sin(angles), jnp.sin(angles)], 1)
    return (cosine_table, sine_table)


def unrotate(gradient, cosine_table, sine_table):
    half_size = gradient.shape[-1] // 2
    scaled = gradient * sine_table
    turned = jnp.concatenate([-scaled[..., half_size:], scaled[..., :half_size]], -1)
    return gradient * cosine_table - turned


def owned_block(partial, owner_row, block_pick, seq_count):
    full_blocks = D // BLOCK
    tail_rows = D - full_blocks * BLOCK
    piece = BLOCK // seq_count
    tail_piece = tail_rows // seq_count
    columns = partial.shape[1]
    main = partial[: full_blocks * BLOCK].reshape(full_blocks, seq_count, piece, columns)
    main = main.transpose(1, 0, 2, 3).reshape(seq_count, full_blocks * piece, columns)
    tail = partial[full_blocks * BLOCK :].reshape(seq_count, tail_piece, columns)
    arranged = jnp.concatenate([main, tail], 1).reshape(-1, columns)
    mine = lax.psum_scatter(arranged, "seq", scatter_dimension=0, tiled=True)
    mine = jnp.concatenate(
        [mine, jnp.zeros((NBLK * piece - mine.shape[0], columns), mine.dtype)], 0
    ).reshape(NBLK, piece, columns)
    destinations = jnp.arange(seq_count, dtype=jnp.int32)
    dest_block = jnp.sum(
        jnp.where(
            owner_row[None, :] == destinations[:, None],
            jnp.arange(NBLK, dtype=jnp.int32)[None, :],
            0,
        ),
        1,
    )
    send = jnp.take(mine, dest_block, axis=0)
    received = lax.all_to_all(send, "seq", 0, 0, tiled=False)
    main_block = received.reshape(BLOCK, columns)
    tail_block = jnp.concatenate(
        [
            received[:, :tail_piece].reshape(tail_piece * seq_count, columns),
            jnp.zeros((BLOCK - tail_piece * seq_count, columns), received.dtype),
        ],
        0,
    )
    return jnp.where(block_pick == full_blocks, tail_block, main_block)


def per_device(inputs, queries, key_rows, values, out_grad, band_start, owners):
    tok_rows = queries.shape[0]
    seq_count = lax.axis_size("seq")
    seq_index = lax.axis_index("seq")
    group_index = lax.axis_index("head")
    tokens_all = tok_rows * seq_count
    earlier_keys, earlier_values = shifted((key_rows, values), "seq", 1)
    gathered_key_rows = jnp.concatenate([earlier_keys, key_rows], 0).reshape(
        2 * tok_rows, KV_DEV, HD
    )
    value_all = jnp.concatenate([earlier_values, values], 0).reshape(2 * tok_rows, KV_DEV, HD)
    query_heads = queries.reshape(tok_rows, KV_DEV, QPK, HD)
    out_heads = out_grad.reshape(tok_rows, KV_DEV, QPK, HD)
    block_rows = min(512, tok_rows)
    span_rows = block_rows + WINDOW
    block_count = tok_rows // block_rows

    def one_block(block_index, state_pair):
        grad_query, grad_keys, grad_values = state_pair
        offset = block_index * block_rows
        query_part = lax.dynamic_slice_in_dim(query_heads, offset, block_rows, 0)
        out_part = lax.dynamic_slice_in_dim(out_heads, offset, block_rows, 0)
        key_start = tok_rows + offset - WINDOW
        key_part = lax.dynamic_slice_in_dim(gathered_key_rows, key_start, span_rows, 0)
        value_part = lax.dynamic_slice_in_dim(value_all, key_start, span_rows, 0)
        band_part = lax.dynamic_slice_in_dim(band_start, offset, block_rows, 0)
        query_pos = seq_index * tok_rows + offset + jnp.arange(block_rows, dtype=jnp.int32)
        key_pos = seq_index * tok_rows + offset - WINDOW + jnp.arange(span_rows, dtype=jnp.int32)
        allowed = (key_pos[None, :] >= band_part[:, None]) & (
            key_pos[None, :] <= query_pos[:, None]
        )
        attention_logits = (
            jnp.einsum("qgrh,kgh->grqk", query_part, key_part, preferred_element_type=jnp.float32)
            * score_scale
        )
        masked = jnp.where(allowed, attention_logits, neg_large)
        row_top = jnp.max(masked, -1, keepdims=True)
        exponent = jnp.where(allowed, jnp.exp(masked - row_top), 0.0)
        attend = exponent / jnp.sum(exponent, -1, keepdims=True)
        attend_low = attend.astype(jnp.bfloat16)
        grad_attend = jnp.einsum(
            "qgrh,kgh->grqk", out_part, value_part, preferred_element_type=jnp.float32
        )
        row_dot = jnp.sum(attend * grad_attend, -1, keepdims=True)
        grad_score = (attend * (grad_attend - row_dot) * score_scale).astype(jnp.bfloat16)
        query_term = jnp.einsum(
            "grqk,kgh->qgrh", grad_score, key_part, preferred_element_type=jnp.float32
        )
        key_term = jnp.einsum(
            "grqk,qgrh->kgh", grad_score, query_part, preferred_element_type=jnp.float32
        )
        value_term = jnp.einsum(
            "grqk,qgrh->kgh", attend_low, out_part, preferred_element_type=jnp.float32
        )
        grad_query = lax.dynamic_update_slice_in_dim(grad_query, query_term, offset, 0)
        grad_keys = lax.dynamic_update_slice_in_dim(
            grad_keys,
            lax.dynamic_slice_in_dim(grad_keys, key_start, span_rows, 0) + key_term,
            key_start,
            0,
        )
        grad_values = lax.dynamic_update_slice_in_dim(
            grad_values,
            lax.dynamic_slice_in_dim(grad_values, key_start, span_rows, 0) + value_term,
            key_start,
            0,
        )
        return (grad_query, grad_keys, grad_values)

    start_state = (
        jnp.zeros((tok_rows, KV_DEV, QPK, HD), jnp.float32),
        jnp.zeros((2 * tok_rows, KV_DEV, HD), jnp.float32),
        jnp.zeros((2 * tok_rows, KV_DEV, HD), jnp.float32),
    )
    grad_query, grad_keys, grad_values = lax.fori_loop(0, block_count, one_block, start_state)
    rim_keys, rim_values = (
        shifted(grad_keys[:tok_rows].astype(jnp.bfloat16), "seq", -1).astype(jnp.float32),
        shifted(grad_values[:tok_rows].astype(jnp.bfloat16), "seq", -1).astype(jnp.float32),
    )
    own_keys = grad_keys[tok_rows:] + rim_keys
    own_values = grad_values[tok_rows:] + rim_values
    positions = seq_index * tok_rows + jnp.arange(tok_rows, dtype=jnp.int32)
    cosine_table, sine_table = rope_tables(positions, HD)
    query_pre = unrotate(
        grad_query.reshape(tok_rows, KV_DEV * QPK, HD),
        cosine_table[:, None, :],
        sine_table[:, None, :],
    )
    key_pre = unrotate(own_keys, cosine_table[:, None, :], sine_table[:, None, :])
    column_grads = jnp.concatenate(
        [
            query_pre.reshape(tok_rows, KV_DEV * QPK * HD),
            key_pre.reshape(tok_rows, KV_DEV * HD),
            own_values.reshape(tok_rows, KV_DEV * HD),
        ],
        1,
    ).astype(jnp.bfloat16)
    column_count = column_grads.shape[1]
    partial_sum = lax.dot_general(
        lax.all_gather(inputs, "head", axis=0, tiled=True),
        column_grads,
        (((0,), (0,)), ((), ())),
        preferred_element_type=jnp.float32,
    )
    owner_row = lax.dynamic_index_in_dim(owners, group_index, 0, keepdims=False)
    is_mine = owner_row == seq_index
    block_pick = jnp.sum(jnp.where(is_mine, jnp.arange(NBLK, dtype=jnp.int32), 0))
    block_part = owned_block(partial_sum.astype(jnp.bfloat16), owner_row, block_pick, seq_count)
    def gram_pair(part_rows):
        left_value = (
            lax.dot_general(
                part_rows, part_rows, (((1,), (1,)), ((), ())), preferred_element_type=jnp.float32
            )
            / tokens_all
        )
        right_value = (
            lax.dot_general(
                part_rows, part_rows, (((0,), (0,)), ((), ())), preferred_element_type=jnp.float32
            )
            / tokens_all
        )
        return (left_value, right_value)

    def nothing(part_rows):
        return (
            jnp.zeros((BLOCK, BLOCK), jnp.float32),
            jnp.zeros((column_count, column_count), jnp.float32),
        )

    left_stat, right_stat = lax.cond(jnp.any(is_mine), gram_pair, nothing, block_part)
    return (left_stat[None, None], right_stat[None, None])


def solution(mesh):
    in_specs = (
        P(("seq", "head"), None),
        P("seq", "head"),
        P("seq", "head"),
        P("seq", "head"),
        P("seq", "head"),
        P("seq"),
        P(),
    )
    out_specs = (P("seq", "head", None, None), P("seq", "head", None, None))
    return jax.shard_map(
        per_device, mesh=mesh, in_specs=in_specs, out_specs=out_specs, check_vma=False
    )
```

```python
import jax
import jax.numpy as jnp
from jax import lax
from jax.sharding import PartitionSpec as P

D = 5376
HD = 128
KV_DEV = 2
QPK = 2
WINDOW = 1024
BLOCK = 1024
NBLK = 6


score_scale = 168.0 ** (-0.5)
rotary_frequency_base = 10000.0
neg_large = -1e30


def shifted(value, axis, steps):
    count = lax.axis_size(axis)
    initial, last = (max(0, -steps), min(count, count - steps))
    return lax.ppermute(value, axis, [(source, source + steps) for source in range(initial, last)])


def rope_tables(positions, head_size):
    half_size = head_size // 2
    frequency = jnp.power(
        rotary_frequency_base, -2.0 * jnp.arange(half_size, dtype=jnp.float32) / head_size
    )
    angles = positions.astype(jnp.float32)[:, None] * frequency[None, :]
    cosine_table = jnp.concatenate([jnp.cos(angles), jnp.cos(angles)], 1)
    sine_table = jnp.concatenate([jnp.sin(angles), jnp.sin(angles)], 1)
    return (cosine_table, sine_table)


def unrotate(gradient, cosine_table, sine_table):
    half_size = gradient.shape[-1] // 2
    scaled = gradient * sine_table
    turned = jnp.concatenate([-scaled[..., half_size:], scaled[..., :half_size]], -1)
    return gradient * cosine_table - turned


def arrange_features(rows, seq_count):
    full_blocks = D // BLOCK
    piece = BLOCK // seq_count
    tail_piece = (D - full_blocks * BLOCK) // seq_count
    count = rows.shape[0]
    main = rows[:, : full_blocks * BLOCK].reshape(count, full_blocks, seq_count, piece)
    main = main.transpose(0, 2, 1, 3).reshape(count, seq_count, full_blocks * piece)
    tail = rows[:, full_blocks * BLOCK :].reshape(count, seq_count, tail_piece)
    return jnp.concatenate([main, tail], 2).reshape(count, D)


def owned_block(arranged, owner_row, block_pick, seq_count, seq_index):
    full_blocks = D // BLOCK
    piece = BLOCK // seq_count
    tail_piece = (D - full_blocks * BLOCK) // seq_count
    columns = arranged.shape[1]
    mine = lax.psum_scatter(arranged, "seq", scatter_dimension=0, tiled=True)
    mine = jnp.concatenate(
        [mine, jnp.zeros((NBLK * piece - mine.shape[0], columns), mine.dtype)], 0
    ).reshape(NBLK, piece, columns)
    destinations = jnp.arange(seq_count, dtype=jnp.int32)
    dest_block = jnp.sum(
        jnp.where(
            owner_row[None, :] == destinations[:, None],
            jnp.arange(NBLK, dtype=jnp.int32)[None, :],
            0,
        ),
        1,
    )
    chunks = []
    for step in range(seq_count):
        target = (seq_index - step) % seq_count
        chunk = lax.dynamic_index_in_dim(
            mine, lax.dynamic_index_in_dim(dest_block, target, 0, keepdims=False), 0, keepdims=False
        )
        if step:
            chunk = lax.ppermute(
                chunk, "seq", [(src, (src - step) % seq_count) for src in range(seq_count)]
            )
        chunks.append(chunk)
    stacked = jnp.stack(chunks, 0)
    doubled = jnp.concatenate([stacked, stacked], 0)
    received = lax.dynamic_slice_in_dim(doubled, seq_count - seq_index, seq_count, 0)
    main_block = received.reshape(BLOCK, columns)
    tail_block = jnp.concatenate(
        [
            received[:, :tail_piece].reshape(tail_piece * seq_count, columns),
            jnp.zeros((BLOCK - tail_piece * seq_count, columns), received.dtype),
        ],
        0,
    )
    return jnp.where(block_pick == full_blocks, tail_block, main_block)

def per_device(inputs, queries, key_rows, values, out_grad, band_start, owners):
    tok_rows = queries.shape[0]
    seq_count = lax.axis_size("seq")
    seq_index = lax.axis_index("seq")
    group_index = lax.axis_index("head")
    tokens_all = tok_rows * seq_count
    earlier_keys, earlier_values = shifted((key_rows, values), "seq", 1)
    gathered_key_rows = jnp.concatenate([earlier_keys, key_rows], 0).reshape(
        2 * tok_rows, KV_DEV, HD
    )
    value_all = jnp.concatenate([earlier_values, values], 0).reshape(2 * tok_rows, KV_DEV, HD)
    query_heads = queries.reshape(tok_rows, KV_DEV, QPK, HD)
    out_heads = out_grad.reshape(tok_rows, KV_DEV, QPK, HD)
    block_rows = min(512, tok_rows)
    span_rows = block_rows + WINDOW
    block_count = tok_rows // block_rows

    def one_block(block_index, state_pair):
        grad_query, grad_keys, grad_values = state_pair
        offset = block_index * block_rows
        query_part = lax.dynamic_slice_in_dim(query_heads, offset, block_rows, 0)
        out_part = lax.dynamic_slice_in_dim(out_heads, offset, block_rows, 0)
        key_start = tok_rows + offset - WINDOW
        key_part = lax.dynamic_slice_in_dim(gathered_key_rows, key_start, span_rows, 0)
        value_part = lax.dynamic_slice_in_dim(value_all, key_start, span_rows, 0)
        band_part = lax.dynamic_slice_in_dim(band_start, offset, block_rows, 0)
        query_pos = seq_index * tok_rows + offset + jnp.arange(block_rows, dtype=jnp.int32)
        key_pos = seq_index * tok_rows + offset - WINDOW + jnp.arange(span_rows, dtype=jnp.int32)
        allowed = (key_pos[None, :] >= band_part[:, None]) & (
            key_pos[None, :] <= query_pos[:, None]
        )
        attention_logits = (
            jnp.einsum("qgrh,kgh->grqk", query_part, key_part, preferred_element_type=jnp.float32)
            * score_scale
        )
        masked = jnp.where(allowed, attention_logits, neg_large)
        row_top = jnp.max(masked, -1, keepdims=True)
        exponent = jnp.where(allowed, jnp.exp(masked - row_top), 0.0)
        attend = exponent / jnp.sum(exponent, -1, keepdims=True)
        attend_low = attend.astype(jnp.bfloat16)
        grad_attend = jnp.einsum(
            "qgrh,kgh->grqk", out_part, value_part, preferred_element_type=jnp.float32
        )
        row_dot = jnp.sum(attend * grad_attend, -1, keepdims=True)
        grad_score = (attend * (grad_attend - row_dot) * score_scale).astype(jnp.bfloat16)
        query_term = jnp.einsum(
            "grqk,kgh->qgrh", grad_score, key_part, preferred_element_type=jnp.float32
        )
        key_term = jnp.einsum(
            "grqk,qgrh->kgh", grad_score, query_part, preferred_element_type=jnp.float32
        )
        value_term = jnp.einsum(
            "grqk,qgrh->kgh", attend_low, out_part, preferred_element_type=jnp.float32
        )
        grad_query = lax.dynamic_update_slice_in_dim(grad_query, query_term, offset, 0)
        grad_keys = lax.dynamic_update_slice_in_dim(
            grad_keys,
            lax.dynamic_slice_in_dim(grad_keys, key_start, span_rows, 0) + key_term,
            key_start,
            0,
        )
        grad_values = lax.dynamic_update_slice_in_dim(
            grad_values,
            lax.dynamic_slice_in_dim(grad_values, key_start, span_rows, 0) + value_term,
            key_start,
            0,
        )
        return (grad_query, grad_keys, grad_values)

    start_state = (
        jnp.zeros((tok_rows, KV_DEV, QPK, HD), jnp.float32),
        jnp.zeros((2 * tok_rows, KV_DEV, HD), jnp.float32),
        jnp.zeros((2 * tok_rows, KV_DEV, HD), jnp.float32),
    )
    grad_query, grad_keys, grad_values = lax.fori_loop(0, block_count, one_block, start_state)
    rim_keys, rim_values = (
        shifted(grad_keys[:tok_rows].astype(jnp.bfloat16), "seq", -1).astype(jnp.float32),
        shifted(grad_values[:tok_rows].astype(jnp.bfloat16), "seq", -1).astype(jnp.float32),
    )
    own_keys = grad_keys[tok_rows:] + rim_keys
    own_values = grad_values[tok_rows:] + rim_values
    positions = seq_index * tok_rows + jnp.arange(tok_rows, dtype=jnp.int32)
    cosine_table, sine_table = rope_tables(positions, HD)
    query_pre = unrotate(
        grad_query.reshape(tok_rows, KV_DEV * QPK, HD),
        cosine_table[:, None, :],
        sine_table[:, None, :],
    )
    key_pre = unrotate(own_keys, cosine_table[:, None, :], sine_table[:, None, :])
    column_grads = jnp.concatenate(
        [
            query_pre.reshape(tok_rows, KV_DEV * QPK * HD),
            key_pre.reshape(tok_rows, KV_DEV * HD),
            own_values.reshape(tok_rows, KV_DEV * HD),
        ],
        1,
    ).astype(jnp.bfloat16)
    column_count = column_grads.shape[1]
    partial_sum = lax.dot_general(
        lax.all_gather(arrange_features(inputs, seq_count), "head", axis=0, tiled=True),
        column_grads,
        (((0,), (0,)), ((), ())),
        preferred_element_type=jnp.float32,
    )
    owner_row = lax.dynamic_index_in_dim(owners, group_index, 0, keepdims=False)
    is_mine = owner_row == seq_index
    block_pick = jnp.sum(jnp.where(is_mine, jnp.arange(NBLK, dtype=jnp.int32), 0))
    block_part = owned_block(
        partial_sum.astype(jnp.bfloat16), owner_row, block_pick, seq_count, seq_index
    )
    def gram_pair(part_rows):
        left_value = (
            lax.dot_general(
                part_rows, part_rows, (((1,), (1,)), ((), ())), preferred_element_type=jnp.float32
            )
            / tokens_all
        )
        right_value = (
            lax.dot_general(
                part_rows, part_rows, (((0,), (0,)), ((), ())), preferred_element_type=jnp.float32
            )
            / tokens_all
        )
        return (left_value, right_value)

    def nothing(part_rows):
        return (
            jnp.zeros((BLOCK, BLOCK), jnp.float32),
            jnp.zeros((column_count, column_count), jnp.float32),
        )

    left_stat, right_stat = lax.cond(jnp.any(is_mine), gram_pair, nothing, block_part)
    return (left_stat[None, None], right_stat[None, None])


def solution(mesh):
    in_specs = (
        P(("seq", "head"), None),
        P("seq", "head"),
        P("seq", "head"),
        P("seq", "head"),
        P("seq", "head"),
        P("seq"),
        P(),
    )
    out_specs = (P("seq", "head", None, None), P("seq", "head", None, None))
    return jax.shard_map(
        per_device, mesh=mesh, in_specs=in_specs, out_specs=out_specs, check_vma=False
    )
```

```python
import jax
import jax.numpy as jnp
from jax import lax
from jax.sharding import PartitionSpec as P

D = 5376
HD = 128
KV_DEV = 2
QPK = 2
WINDOW = 1024
BLOCK = 1024
NBLK = 6


score_scale = 168.0 ** (-0.5)
rotary_frequency_base = 10000.0
neg_large = -1e30


def shifted(value, axis, steps):
    count = lax.axis_size(axis)
    initial, last = (max(0, -steps), min(count, count - steps))
    return lax.ppermute(value, axis, [(source, source + steps) for source in range(initial, last)])


def rope_tables(positions, head_size):
    half_size = head_size // 2
    frequency = jnp.power(
        rotary_frequency_base, -2.0 * jnp.arange(half_size, dtype=jnp.float32) / head_size
    )
    angles = positions.astype(jnp.float32)[:, None] * frequency[None, :]
    cosine_table = jnp.concatenate([jnp.cos(angles), jnp.cos(angles)], 1)
    sine_table = jnp.concatenate([jnp.sin(angles), jnp.sin(angles)], 1)
    return (cosine_table, sine_table)


def unrotate(gradient, cosine_table, sine_table):
    half_size = gradient.shape[-1] // 2
    scaled = gradient * sine_table
    turned = jnp.concatenate([-scaled[..., half_size:], scaled[..., :half_size]], -1)
    return gradient * cosine_table - turned


def arrange_features(rows, seq_count):
    full_blocks = D // BLOCK
    piece = BLOCK // seq_count
    tail_piece = (D - full_blocks * BLOCK) // seq_count
    count = rows.shape[0]
    main = rows[:, : full_blocks * BLOCK].reshape(count, full_blocks, seq_count, piece)
    main = main.transpose(0, 2, 1, 3).reshape(count, seq_count, full_blocks * piece)
    tail = rows[:, full_blocks * BLOCK :].reshape(count, seq_count, tail_piece)
    return jnp.concatenate([main, tail], 2).reshape(count, D)


def owned_block(arranged, owner_row, block_pick, seq_count):
    full_blocks = D // BLOCK
    piece = BLOCK // seq_count
    tail_piece = (D - full_blocks * BLOCK) // seq_count
    columns = arranged.shape[1]
    mine = lax.psum_scatter(arranged, "seq", scatter_dimension=0, tiled=True)
    mine = jnp.concatenate(
        [mine, jnp.zeros((NBLK * piece - mine.shape[0], columns), mine.dtype)], 0
    ).reshape(NBLK, piece, columns)
    destinations = jnp.arange(seq_count, dtype=jnp.int32)
    dest_block = jnp.sum(
        jnp.where(
            owner_row[None, :] == destinations[:, None],
            jnp.arange(NBLK, dtype=jnp.int32)[None, :],
            0,
        ),
        1,
    )
    send = jnp.take(mine, dest_block, axis=0)
    received = lax.all_to_all(send, "seq", 0, 0, tiled=False)
    main_block = received.reshape(BLOCK, columns)
    tail_block = jnp.concatenate(
        [
            received[:, :tail_piece].reshape(tail_piece * seq_count, columns),
            jnp.zeros((BLOCK - tail_piece * seq_count, columns), received.dtype),
        ],
        0,
    )
    return jnp.where(block_pick == full_blocks, tail_block, main_block)

def per_device(inputs, queries, key_rows, values, out_grad, band_start, owners):
    tok_rows = queries.shape[0]
    seq_count = lax.axis_size("seq")
    seq_index = lax.axis_index("seq")
    group_index = lax.axis_index("head")
    tokens_all = tok_rows * seq_count
    earlier_keys, earlier_values = shifted((key_rows, values), "seq", 1)
    gathered_key_rows = jnp.concatenate([earlier_keys, key_rows], 0).reshape(
        2 * tok_rows, KV_DEV, HD
    )
    value_all = jnp.concatenate([earlier_values, values], 0).reshape(2 * tok_rows, KV_DEV, HD)
    query_heads = queries.reshape(tok_rows, KV_DEV, QPK, HD)
    out_heads = out_grad.reshape(tok_rows, KV_DEV, QPK, HD)
    block_rows = min(512, tok_rows)
    span_rows = block_rows + WINDOW
    block_count = tok_rows // block_rows

    def one_block(block_index, state_pair):
        grad_query, grad_keys, grad_values = state_pair
        offset = block_index * block_rows
        query_part = lax.dynamic_slice_in_dim(query_heads, offset, block_rows, 0)
        out_part = lax.dynamic_slice_in_dim(out_heads, offset, block_rows, 0)
        key_start = tok_rows + offset - WINDOW
        key_part = lax.dynamic_slice_in_dim(gathered_key_rows, key_start, span_rows, 0)
        value_part = lax.dynamic_slice_in_dim(value_all, key_start, span_rows, 0)
        band_part = lax.dynamic_slice_in_dim(band_start, offset, block_rows, 0)
        query_pos = seq_index * tok_rows + offset + jnp.arange(block_rows, dtype=jnp.int32)
        key_pos = seq_index * tok_rows + offset - WINDOW + jnp.arange(span_rows, dtype=jnp.int32)
        allowed = (key_pos[None, :] >= band_part[:, None]) & (
            key_pos[None, :] <= query_pos[:, None]
        )
        attention_logits = (
            jnp.einsum("qgrh,kgh->grqk", query_part, key_part, preferred_element_type=jnp.float32)
            * score_scale
        )
        masked = jnp.where(allowed, attention_logits, neg_large)
        row_top = jnp.max(masked, -1, keepdims=True)
        exponent = jnp.where(allowed, jnp.exp(masked - row_top), 0.0)
        attend = exponent / jnp.sum(exponent, -1, keepdims=True)
        attend_low = attend.astype(jnp.bfloat16)
        grad_attend = jnp.einsum(
            "qgrh,kgh->grqk", out_part, value_part, preferred_element_type=jnp.float32
        )
        row_dot = jnp.sum(attend * grad_attend, -1, keepdims=True)
        grad_score = (attend * (grad_attend - row_dot) * score_scale).astype(jnp.bfloat16)
        query_term = jnp.einsum(
            "grqk,kgh->qgrh", grad_score, key_part, preferred_element_type=jnp.float32
        )
        key_term = jnp.einsum(
            "grqk,qgrh->kgh", grad_score, query_part, preferred_element_type=jnp.float32
        )
        value_term = jnp.einsum(
            "grqk,qgrh->kgh", attend_low, out_part, preferred_element_type=jnp.float32
        )
        grad_query = lax.dynamic_update_slice_in_dim(grad_query, query_term, offset, 0)
        grad_keys = lax.dynamic_update_slice_in_dim(
            grad_keys,
            lax.dynamic_slice_in_dim(grad_keys, key_start, span_rows, 0) + key_term,
            key_start,
            0,
        )
        grad_values = lax.dynamic_update_slice_in_dim(
            grad_values,
            lax.dynamic_slice_in_dim(grad_values, key_start, span_rows, 0) + value_term,
            key_start,
            0,
        )
        return (grad_query, grad_keys, grad_values)

    start_state = (
        jnp.zeros((tok_rows, KV_DEV, QPK, HD), jnp.float32),
        jnp.zeros((2 * tok_rows, KV_DEV, HD), jnp.float32),
        jnp.zeros((2 * tok_rows, KV_DEV, HD), jnp.float32),
    )
    grad_query, grad_keys, grad_values = lax.fori_loop(0, block_count, one_block, start_state)
    rim_keys, rim_values = (
        shifted(grad_keys[:tok_rows].astype(jnp.bfloat16), "seq", -1).astype(jnp.float32),
        shifted(grad_values[:tok_rows].astype(jnp.bfloat16), "seq", -1).astype(jnp.float32),
    )
    own_keys = grad_keys[tok_rows:] + rim_keys
    own_values = grad_values[tok_rows:] + rim_values
    positions = seq_index * tok_rows + jnp.arange(tok_rows, dtype=jnp.int32)
    cosine_table, sine_table = rope_tables(positions, HD)
    query_pre = unrotate(
        grad_query.reshape(tok_rows, KV_DEV * QPK, HD),
        cosine_table[:, None, :],
        sine_table[:, None, :],
    )
    key_pre = unrotate(own_keys, cosine_table[:, None, :], sine_table[:, None, :])
    column_grads = jnp.concatenate(
        [
            query_pre.reshape(tok_rows, KV_DEV * QPK * HD),
            key_pre.reshape(tok_rows, KV_DEV * HD),
            own_values.reshape(tok_rows, KV_DEV * HD),
        ],
        1,
    ).astype(jnp.bfloat16)
    column_count = column_grads.shape[1]
    partial_sum = lax.dot_general(
        lax.all_gather(arrange_features(inputs, seq_count), "head", axis=0, tiled=True),
        column_grads,
        (((0,), (0,)), ((), ())),
        preferred_element_type=jnp.float32,
    )
    owner_row = lax.dynamic_index_in_dim(owners, group_index, 0, keepdims=False)
    is_mine = owner_row == seq_index
    block_pick = jnp.sum(jnp.where(is_mine, jnp.arange(NBLK, dtype=jnp.int32), 0))
    block_part = owned_block(partial_sum.astype(jnp.bfloat16), owner_row, block_pick, seq_count)
    def gram_pair(part_rows):
        left_value = (
            lax.dot_general(
                part_rows, part_rows, (((1,), (1,)), ((), ())), preferred_element_type=jnp.float32
            )
            / tokens_all
        )
        right_value = (
            lax.dot_general(
                part_rows, part_rows, (((0,), (0,)), ((), ())), preferred_element_type=jnp.float32
            )
            / tokens_all
        )
        return (left_value, right_value)

    def nothing(part_rows):
        return (
            jnp.zeros((BLOCK, BLOCK), jnp.float32),
            jnp.zeros((column_count, column_count), jnp.float32),
        )

    left_stat, right_stat = lax.cond(jnp.any(is_mine), gram_pair, nothing, block_part)
    return (left_stat[None, None], right_stat[None, None])


def solution(mesh):
    in_specs = (
        P(("seq", "head"), None),
        P("seq", "head"),
        P("seq", "head"),
        P("seq", "head"),
        P("seq", "head"),
        P("seq"),
        P(),
    )
    out_specs = (P("seq", "head", None, None), P("seq", "head", None, None))
    return jax.shard_map(
        per_device, mesh=mesh, in_specs=in_specs, out_specs=out_specs, check_vma=False
    )
```

```python
import jax
import jax.numpy as jnp
from jax import lax
from jax.sharding import PartitionSpec as P
from jax.experimental import pallas as pl
from jax.experimental.pallas import tpu as pltpu

D = 5376
HD = 128
KV_DEV = 2
QPK = 2
WINDOW = 1024
BLOCK = 1024
NBLK = 6


score_scale = 168.0 ** (-0.5)
rotary_frequency_base = 10000.0
neg_large = -1e30
QBLK = 256


def attention_kernel(band_ref, q_ref, do_ref, k_ref, v_ref, dq_ref, dk_ref, dv_ref):
    tok_rows = q_ref.shape[0]
    span = QBLK + WINDOW
    dk_ref[...] = jnp.zeros(dk_ref.shape, jnp.float32)
    dv_ref[...] = jnp.zeros(dv_ref.shape, jnp.float32)
    def one_block(qb, carry):
        q0 = pl.multiple_of(qb * QBLK, QBLK)
        band = band_ref[pl.ds(q0, QBLK), :]
        band = jnp.concatenate([band, band], 0)
        col = lax.broadcasted_iota(jnp.int32, (QPK * QBLK, span), 1)
        row = lax.broadcasted_iota(jnp.int32, (QPK * QBLK, span), 0) % QBLK
        allowed = (col + q0 >= band) & (col <= row + WINDOW)
        for g in range(KV_DEV):
            base = g * QPK * HD
            qs = jnp.concatenate(
                [q_ref[pl.ds(q0, QBLK), base + r * HD:base + (r + 1) * HD] for r in range(QPK)], 0)
            dos = jnp.concatenate(
                [do_ref[pl.ds(q0, QBLK), base + r * HD:base + (r + 1) * HD] for r in range(QPK)], 0)
            keys = k_ref[pl.ds(q0, span), g * HD:(g + 1) * HD]
            vals = v_ref[pl.ds(q0, span), g * HD:(g + 1) * HD]
            logits = lax.dot_general(qs, keys, (((1,), (1,)), ((), ())),
                                     preferred_element_type=jnp.float32) * score_scale
            masked = jnp.where(allowed, logits, neg_large)
            top = jnp.max(masked, -1, keepdims=True)
            expo = jnp.where(allowed, jnp.exp(masked - top), 0.0)
            attend = expo / jnp.sum(expo, -1, keepdims=True)
            grad_attend = lax.dot_general(dos, vals, (((1,), (1,)), ((), ())),
                                          preferred_element_type=jnp.float32)
            row_dot = jnp.sum(attend * grad_attend, -1, keepdims=True)
            grad_score = (attend * (grad_attend - row_dot) * score_scale).astype(jnp.bfloat16)
            dqs = jnp.dot(grad_score, keys, preferred_element_type=jnp.float32)
            for r in range(QPK):
                dq_ref[pl.ds(q0, QBLK), base + r * HD:base + (r + 1) * HD] = dqs[r * QBLK:(r + 1) * QBLK]
            dk_ref[pl.ds(q0, span), g * HD:(g + 1) * HD] += lax.dot_general(
                grad_score, qs, (((0,), (0,)), ((), ())), preferred_element_type=jnp.float32)
            dv_ref[pl.ds(q0, span), g * HD:(g + 1) * HD] += lax.dot_general(
                attend.astype(jnp.bfloat16), dos, (((0,), (0,)), ((), ())),
                preferred_element_type=jnp.float32)
        return carry

    lax.fori_loop(0, tok_rows // QBLK, one_block, 0)


def attention_backward(band_rel, queries, out_grad, key_all, value_all):
    tok_rows = queries.shape[0]
    vmem = pl.BlockSpec(memory_space=pltpu.VMEM)
    return pl.pallas_call(
        attention_kernel,
        out_shape=(
            jax.ShapeDtypeStruct(queries.shape, jnp.float32),
            jax.ShapeDtypeStruct(key_all.shape, jnp.float32),
            jax.ShapeDtypeStruct(value_all.shape, jnp.float32),
        ),
        in_specs=[vmem] * 5,
        out_specs=(vmem, vmem, vmem),
    )(band_rel.reshape(tok_rows, 1), queries, out_grad, key_all, value_all)


def shifted(value, axis, steps):
    count = lax.axis_size(axis)
    initial, last = (max(0, -steps), min(count, count - steps))
    return lax.ppermute(value, axis, [(source, source + steps) for source in range(initial, last)])


def rope_tables(positions, head_size):
    half_size = head_size // 2
    frequency = jnp.power(
        rotary_frequency_base, -2.0 * jnp.arange(half_size, dtype=jnp.float32) / head_size
    )
    angles = positions.astype(jnp.float32)[:, None] * frequency[None, :]
    cosine_table = jnp.concatenate([jnp.cos(angles), jnp.cos(angles)], 1)
    sine_table = jnp.concatenate([jnp.sin(angles), jnp.sin(angles)], 1)
    return (cosine_table, sine_table)


def unrotate(gradient, cosine_table, sine_table):
    half_size = gradient.shape[-1] // 2
    scaled = gradient * sine_table
    turned = jnp.concatenate([-scaled[..., half_size:], scaled[..., :half_size]], -1)
    return gradient * cosine_table - turned


def arrange_features(rows, seq_count):
    full_blocks = D // BLOCK
    piece = BLOCK // seq_count
    tail_piece = (D - full_blocks * BLOCK) // seq_count
    count = rows.shape[0]
    main = rows[:, : full_blocks * BLOCK].reshape(count, full_blocks, seq_count, piece)
    main = main.transpose(0, 2, 1, 3).reshape(count, seq_count, full_blocks * piece)
    tail = rows[:, full_blocks * BLOCK :].reshape(count, seq_count, tail_piece)
    return jnp.concatenate([main, tail], 2).reshape(count, D)


def owned_block(arranged, owner_row, block_pick, seq_count):
    full_blocks = D // BLOCK
    piece = BLOCK // seq_count
    tail_piece = (D - full_blocks * BLOCK) // seq_count
    columns = arranged.shape[1]
    mine = lax.psum_scatter(arranged, "seq", scatter_dimension=0, tiled=True)
    mine = jnp.concatenate(
        [mine, jnp.zeros((NBLK * piece - mine.shape[0], columns), mine.dtype)], 0
    ).reshape(NBLK, piece, columns)
    destinations = jnp.arange(seq_count, dtype=jnp.int32)
    dest_block = jnp.sum(
        jnp.where(
            owner_row[None, :] == destinations[:, None],
            jnp.arange(NBLK, dtype=jnp.int32)[None, :],
            0,
        ),
        1,
    )
    send = jnp.take(mine, dest_block, axis=0)
    received = lax.all_to_all(send, "seq", 0, 0, tiled=False)
    main_block = received.reshape(BLOCK, columns)
    tail_block = jnp.concatenate(
        [
            received[:, :tail_piece].reshape(tail_piece * seq_count, columns),
            jnp.zeros((BLOCK - tail_piece * seq_count, columns), received.dtype),
        ],
        0,
    )
    return jnp.where(block_pick == full_blocks, tail_block, main_block)

def per_device(inputs, queries, key_rows, values, out_grad, band_start, owners):
    tok_rows = queries.shape[0]
    seq_count = lax.axis_size("seq")
    seq_index = lax.axis_index("seq")
    group_index = lax.axis_index("head")
    tokens_all = tok_rows * seq_count
    earlier_keys, earlier_values = shifted((key_rows, values), "seq", 1)
    key_all = jnp.concatenate([earlier_keys, key_rows], 0)
    value_all = jnp.concatenate([earlier_values, values], 0)
    band_rel = band_start - (seq_index * tok_rows - WINDOW)
    grad_query, grad_keys, grad_values = attention_backward(
        band_rel, queries, out_grad, key_all, value_all
    )
    grad_keys = grad_keys.reshape(2 * tok_rows, KV_DEV, HD)
    grad_values = grad_values.reshape(2 * tok_rows, KV_DEV, HD)
    rim_keys, rim_values = (
        shifted(grad_keys[:tok_rows].astype(jnp.bfloat16), "seq", -1).astype(jnp.float32),
        shifted(grad_values[:tok_rows].astype(jnp.bfloat16), "seq", -1).astype(jnp.float32),
    )
    own_keys = grad_keys[tok_rows:] + rim_keys
    own_values = grad_values[tok_rows:] + rim_values
    positions = seq_index * tok_rows + jnp.arange(tok_rows, dtype=jnp.int32)
    cosine_table, sine_table = rope_tables(positions, HD)
    query_pre = unrotate(
        grad_query.reshape(tok_rows, KV_DEV * QPK, HD),
        cosine_table[:, None, :],
        sine_table[:, None, :],
    )
    key_pre = unrotate(own_keys, cosine_table[:, None, :], sine_table[:, None, :])
    column_grads = jnp.concatenate(
        [
            query_pre.reshape(tok_rows, KV_DEV * QPK * HD),
            key_pre.reshape(tok_rows, KV_DEV * HD),
            own_values.reshape(tok_rows, KV_DEV * HD),
        ],
        1,
    ).astype(jnp.bfloat16)
    column_count = column_grads.shape[1]
    partial_sum = lax.dot_general(
        lax.all_gather(arrange_features(inputs, seq_count), "head", axis=0, tiled=True),
        column_grads,
        (((0,), (0,)), ((), ())),
        preferred_element_type=jnp.float32,
    )
    owner_row = lax.dynamic_index_in_dim(owners, group_index, 0, keepdims=False)
    is_mine = owner_row == seq_index
    block_pick = jnp.sum(jnp.where(is_mine, jnp.arange(NBLK, dtype=jnp.int32), 0))
    block_part = owned_block(partial_sum.astype(jnp.bfloat16), owner_row, block_pick, seq_count)
    def gram_pair(part_rows):
        left_value = (
            lax.dot_general(
                part_rows, part_rows, (((1,), (1,)), ((), ())), preferred_element_type=jnp.float32
            )
            / tokens_all
        )
        right_value = (
            lax.dot_general(
                part_rows, part_rows, (((0,), (0,)), ((), ())), preferred_element_type=jnp.float32
            )
            / tokens_all
        )
        return (left_value, right_value)

    def nothing(part_rows):
        return (
            jnp.zeros((BLOCK, BLOCK), jnp.float32),
            jnp.zeros((column_count, column_count), jnp.float32),
        )

    left_stat, right_stat = lax.cond(jnp.any(is_mine), gram_pair, nothing, block_part)
    return (left_stat[None, None], right_stat[None, None])


def solution(mesh):
    in_specs = (
        P(("seq", "head"), None),
        P("seq", "head"),
        P("seq", "head"),
        P("seq", "head"),
        P("seq", "head"),
        P("seq"),
        P(),
    )
    out_specs = (P("seq", "head", None, None), P("seq", "head", None, None))
    return jax.shard_map(
        per_device, mesh=mesh, in_specs=in_specs, out_specs=out_specs, check_vma=False
    )
```

```python
import jax
import jax.numpy as jnp
from jax import lax
from jax.sharding import PartitionSpec as P
from jax.experimental import pallas as pl
from jax.experimental.pallas import tpu as pltpu

D = 5376
HD = 128
KV_DEV = 2
QPK = 2
WINDOW = 1024
BLOCK = 1024
NBLK = 6


score_scale = 168.0 ** (-0.5)
rotary_frequency_base = 10000.0
neg_large = -1e30
QBLK = 256


def attention_kernel(band_ref, q_ref, do_ref, k_ref, v_ref, dq_ref, dk_ref, dv_ref):
    tok_rows = q_ref.shape[0]
    span = QBLK + WINDOW
    dk_ref[...] = jnp.zeros(dk_ref.shape, jnp.float32)
    dv_ref[...] = jnp.zeros(dv_ref.shape, jnp.float32)
    def one_block(qb, carry):
        q0 = pl.multiple_of(qb * QBLK, QBLK)
        band = band_ref[pl.ds(q0, QBLK), :]
        band = jnp.concatenate([band, band], 0)
        col = lax.broadcasted_iota(jnp.int32, (QPK * QBLK, span), 1)
        row = lax.broadcasted_iota(jnp.int32, (QPK * QBLK, span), 0) % QBLK
        allowed = (col + q0 >= band) & (col <= row + WINDOW)
        for g in range(KV_DEV):
            base = g * QPK * HD
            qs = jnp.concatenate(
                [q_ref[pl.ds(q0, QBLK), base + r * HD:base + (r + 1) * HD] for r in range(QPK)], 0)
            dos = jnp.concatenate(
                [do_ref[pl.ds(q0, QBLK), base + r * HD:base + (r + 1) * HD] for r in range(QPK)], 0)
            keys = k_ref[pl.ds(q0, span), g * HD:(g + 1) * HD]
            vals = v_ref[pl.ds(q0, span), g * HD:(g + 1) * HD]
            logits = lax.dot_general(qs, keys, (((1,), (1,)), ((), ())),
                                     preferred_element_type=jnp.float32) * score_scale
            masked = jnp.where(allowed, logits, neg_large)
            top = jnp.max(masked, -1, keepdims=True)
            expo = jnp.where(allowed, jnp.exp(masked - top), 0.0)
            attend = expo / jnp.sum(expo, -1, keepdims=True)
            grad_attend = lax.dot_general(dos, vals, (((1,), (1,)), ((), ())),
                                          preferred_element_type=jnp.float32)
            row_dot = jnp.sum(attend * grad_attend, -1, keepdims=True)
            grad_score = (attend * (grad_attend - row_dot) * score_scale).astype(jnp.bfloat16)
            dqs = jnp.dot(grad_score, keys, preferred_element_type=jnp.float32)
            for r in range(QPK):
                dq_ref[pl.ds(q0, QBLK), base + r * HD:base + (r + 1) * HD] = dqs[r * QBLK:(r + 1) * QBLK]
            dk_ref[pl.ds(q0, span), g * HD:(g + 1) * HD] += lax.dot_general(
                grad_score, qs, (((0,), (0,)), ((), ())), preferred_element_type=jnp.float32)
            dv_ref[pl.ds(q0, span), g * HD:(g + 1) * HD] += lax.dot_general(
                attend.astype(jnp.bfloat16), dos, (((0,), (0,)), ((), ())),
                preferred_element_type=jnp.float32)
        return carry

    lax.fori_loop(0, tok_rows // QBLK, one_block, 0)


def attention_backward(band_rel, queries, out_grad, key_all, value_all):
    tok_rows = queries.shape[0]
    vmem = pl.BlockSpec(memory_space=pltpu.VMEM)
    return pl.pallas_call(
        attention_kernel,
        out_shape=(
            jax.ShapeDtypeStruct(queries.shape, jnp.float32),
            jax.ShapeDtypeStruct(key_all.shape, jnp.float32),
            jax.ShapeDtypeStruct(value_all.shape, jnp.float32),
        ),
        in_specs=[vmem] * 5,
        out_specs=(vmem, vmem, vmem),
    )(band_rel.reshape(tok_rows, 1), queries, out_grad, key_all, value_all)


def shifted(value, axis, steps):
    count = lax.axis_size(axis)
    initial, last = (max(0, -steps), min(count, count - steps))
    return lax.ppermute(value, axis, [(source, source + steps) for source in range(initial, last)])


def rope_tables(positions, head_size):
    half_size = head_size // 2
    frequency = jnp.power(
        rotary_frequency_base, -2.0 * jnp.arange(half_size, dtype=jnp.float32) / head_size
    )
    angles = positions.astype(jnp.float32)[:, None] * frequency[None, :]
    cosine_table = jnp.concatenate([jnp.cos(angles), jnp.cos(angles)], 1)
    sine_table = jnp.concatenate([jnp.sin(angles), jnp.sin(angles)], 1)
    return (cosine_table, sine_table)


def unrotate(gradient, cosine_table, sine_table):
    half_size = gradient.shape[-1] // 2
    scaled = gradient * sine_table
    turned = jnp.concatenate([-scaled[..., half_size:], scaled[..., :half_size]], -1)
    return gradient * cosine_table - turned


def arrange_features(rows, seq_count):
    full_blocks = D // BLOCK
    piece = BLOCK // seq_count
    tail_piece = (D - full_blocks * BLOCK) // seq_count
    count = rows.shape[0]
    main = rows[:, : full_blocks * BLOCK].reshape(count, full_blocks, seq_count, piece)
    main = main.transpose(0, 2, 1, 3).reshape(count, seq_count, full_blocks * piece)
    tail = rows[:, full_blocks * BLOCK :].reshape(count, seq_count, tail_piece)
    return jnp.concatenate([main, tail], 2).reshape(count, D)


def owned_block(mine, owner_row, block_pick, seq_count):
    full_blocks = D // BLOCK
    piece = BLOCK // seq_count
    tail_piece = (D - full_blocks * BLOCK) // seq_count
    columns = mine.shape[1]
    mine = jnp.concatenate(
        [mine, jnp.zeros((NBLK * piece - mine.shape[0], columns), mine.dtype)], 0
    ).reshape(NBLK, piece, columns)
    destinations = jnp.arange(seq_count, dtype=jnp.int32)
    dest_block = jnp.sum(
        jnp.where(
            owner_row[None, :] == destinations[:, None],
            jnp.arange(NBLK, dtype=jnp.int32)[None, :],
            0,
        ),
        1,
    )
    send = jnp.take(mine, dest_block, axis=0)
    received = lax.all_to_all(send, "seq", 0, 0, tiled=False)
    main_block = received.reshape(BLOCK, columns)
    tail_block = jnp.concatenate(
        [
            received[:, :tail_piece].reshape(tail_piece * seq_count, columns),
            jnp.zeros((BLOCK - tail_piece * seq_count, columns), received.dtype),
        ],
        0,
    )
    return jnp.where(block_pick == full_blocks, tail_block, main_block)

def per_device(inputs, queries, key_rows, values, out_grad, band_start, owners):
    tok_rows = queries.shape[0]
    seq_count = lax.axis_size("seq")
    seq_index = lax.axis_index("seq")
    group_index = lax.axis_index("head")
    tokens_all = tok_rows * seq_count
    earlier_keys, earlier_values = shifted((key_rows, values), "seq", 1)
    key_all = jnp.concatenate([earlier_keys, key_rows], 0)
    value_all = jnp.concatenate([earlier_values, values], 0)
    band_rel = band_start - (seq_index * tok_rows - WINDOW)
    grad_query, grad_keys, grad_values = attention_backward(
        band_rel, queries, out_grad, key_all, value_all
    )
    grad_keys = grad_keys.reshape(2 * tok_rows, KV_DEV, HD)
    grad_values = grad_values.reshape(2 * tok_rows, KV_DEV, HD)
    rim_keys, rim_values = (
        shifted(grad_keys[:tok_rows].astype(jnp.bfloat16), "seq", -1).astype(jnp.float32),
        shifted(grad_values[:tok_rows].astype(jnp.bfloat16), "seq", -1).astype(jnp.float32),
    )
    own_keys = grad_keys[tok_rows:] + rim_keys
    own_values = grad_values[tok_rows:] + rim_values
    positions = seq_index * tok_rows + jnp.arange(tok_rows, dtype=jnp.int32)
    cosine_table, sine_table = rope_tables(positions, HD)
    query_pre = unrotate(
        grad_query.reshape(tok_rows, KV_DEV * QPK, HD),
        cosine_table[:, None, :],
        sine_table[:, None, :],
    )
    key_pre = unrotate(own_keys, cosine_table[:, None, :], sine_table[:, None, :])
    column_grads = jnp.concatenate(
        [
            query_pre.reshape(tok_rows, KV_DEV * QPK * HD),
            key_pre.reshape(tok_rows, KV_DEV * HD),
            own_values.reshape(tok_rows, KV_DEV * HD),
        ],
        1,
    ).astype(jnp.bfloat16)
    column_count = column_grads.shape[1]
    arranged = arrange_features(inputs, seq_count).reshape(inputs.shape[0], seq_count, -1)
    half = arranged.shape[2] // 2
    pieces = []
    for part in (arranged[:, :, :half], arranged[:, :, half:]):
        gathered = lax.all_gather(part.reshape(inputs.shape[0], -1), "head", axis=0, tiled=True)
        partial = lax.dot_general(
            gathered, column_grads, (((0,), (0,)), ((), ())), preferred_element_type=jnp.float32
        )
        pieces.append(
            lax.psum_scatter(partial.astype(jnp.bfloat16), "seq", scatter_dimension=0, tiled=True)
        )
    mine = jnp.concatenate(pieces, 0)
    owner_row = lax.dynamic_index_in_dim(owners, group_index, 0, keepdims=False)
    is_mine = owner_row == seq_index
    block_pick = jnp.sum(jnp.where(is_mine, jnp.arange(NBLK, dtype=jnp.int32), 0))
    block_part = owned_block(mine, owner_row, block_pick, seq_count)
    def gram_pair(part_rows):
        left_value = (
            lax.dot_general(
                part_rows, part_rows, (((1,), (1,)), ((), ())), preferred_element_type=jnp.float32
            )
            / tokens_all
        )
        right_value = (
            lax.dot_general(
                part_rows, part_rows, (((0,), (0,)), ((), ())), preferred_element_type=jnp.float32
            )
            / tokens_all
        )
        return (left_value, right_value)

    def nothing(part_rows):
        return (
            jnp.zeros((BLOCK, BLOCK), jnp.float32),
            jnp.zeros((column_count, column_count), jnp.float32),
        )

    left_stat, right_stat = lax.cond(jnp.any(is_mine), gram_pair, nothing, block_part)
    return (left_stat[None, None], right_stat[None, None])


def solution(mesh):
    in_specs = (
        P(("seq", "head"), None),
        P("seq", "head"),
        P("seq", "head"),
        P("seq", "head"),
        P("seq", "head"),
        P("seq"),
        P(),
    )
    out_specs = (P("seq", "head", None, None), P("seq", "head", None, None))
    return jax.shard_map(
        per_device, mesh=mesh, in_specs=in_specs, out_specs=out_specs, check_vma=False
    )
```

```python
import jax
import jax.numpy as jnp
from jax import lax
from jax.sharding import PartitionSpec as P
from jax.experimental import pallas as pl
from jax.experimental.pallas import tpu as pltpu

D = 5376
HD = 128
KV_DEV = 2
QPK = 2
WINDOW = 1024
BLOCK = 1024
NBLK = 6


score_scale = 168.0 ** (-0.5)
rotary_frequency_base = 10000.0
neg_large = -1e30
QBLK = 256


def attention_kernel(band_ref, q_ref, do_ref, k_ref, v_ref, dq_ref, dk_ref, dv_ref):
    tok_rows = q_ref.shape[0]
    span = QBLK + WINDOW
    dk_ref[...] = jnp.zeros(dk_ref.shape, jnp.float32)
    dv_ref[...] = jnp.zeros(dv_ref.shape, jnp.float32)
    def one_block(qb, carry):
        q0 = pl.multiple_of(qb * QBLK, QBLK)
        band = band_ref[pl.ds(q0, QBLK), :]
        band = jnp.concatenate([band, band], 0)
        col = lax.broadcasted_iota(jnp.int32, (QPK * QBLK, span), 1)
        row = lax.broadcasted_iota(jnp.int32, (QPK * QBLK, span), 0) % QBLK
        allowed = (col + q0 >= band) & (col <= row + WINDOW)
        for g in range(KV_DEV):
            base = g * QPK * HD
            qs = jnp.concatenate(
                [q_ref[pl.ds(q0, QBLK), base + r * HD:base + (r + 1) * HD] for r in range(QPK)], 0)
            dos = jnp.concatenate(
                [do_ref[pl.ds(q0, QBLK), base + r * HD:base + (r + 1) * HD] for r in range(QPK)], 0)
            keys = k_ref[pl.ds(q0, span), g * HD:(g + 1) * HD]
            vals = v_ref[pl.ds(q0, span), g * HD:(g + 1) * HD]
            logits = lax.dot_general(qs, keys, (((1,), (1,)), ((), ())),
                                     preferred_element_type=jnp.float32) * score_scale
            masked = jnp.where(allowed, logits, neg_large)
            top = jnp.max(masked, -1, keepdims=True)
            expo = jnp.where(allowed, jnp.exp(masked - top), 0.0)
            attend = expo / jnp.sum(expo, -1, keepdims=True)
            grad_attend = lax.dot_general(dos, vals, (((1,), (1,)), ((), ())),
                                          preferred_element_type=jnp.float32)
            row_dot = jnp.sum(attend * grad_attend, -1, keepdims=True)
            grad_score = (attend * (grad_attend - row_dot) * score_scale).astype(jnp.bfloat16)
            dqs = jnp.dot(grad_score, keys, preferred_element_type=jnp.float32)
            for r in range(QPK):
                dq_ref[pl.ds(q0, QBLK), base + r * HD:base + (r + 1) * HD] = dqs[r * QBLK:(r + 1) * QBLK]
            dk_ref[pl.ds(q0, span), g * HD:(g + 1) * HD] += lax.dot_general(
                grad_score, qs, (((0,), (0,)), ((), ())), preferred_element_type=jnp.float32)
            dv_ref[pl.ds(q0, span), g * HD:(g + 1) * HD] += lax.dot_general(
                attend.astype(jnp.bfloat16), dos, (((0,), (0,)), ((), ())),
                preferred_element_type=jnp.float32)
        return carry

    lax.fori_loop(0, tok_rows // QBLK, one_block, 0)


def attention_backward(band_rel, queries, out_grad, key_all, value_all):
    tok_rows = queries.shape[0]
    vmem = pl.BlockSpec(memory_space=pltpu.VMEM)
    return pl.pallas_call(
        attention_kernel,
        out_shape=(
            jax.ShapeDtypeStruct(queries.shape, jnp.float32),
            jax.ShapeDtypeStruct(key_all.shape, jnp.float32),
            jax.ShapeDtypeStruct(value_all.shape, jnp.float32),
        ),
        in_specs=[vmem] * 5,
        out_specs=(vmem, vmem, vmem),
    )(band_rel.reshape(tok_rows, 1), queries, out_grad, key_all, value_all)


def shifted(value, axis, steps):
    count = lax.axis_size(axis)
    initial, last = (max(0, -steps), min(count, count - steps))
    return lax.ppermute(value, axis, [(source, source + steps) for source in range(initial, last)])


def rope_tables(positions, head_size):
    half_size = head_size // 2
    frequency = jnp.power(
        rotary_frequency_base, -2.0 * jnp.arange(half_size, dtype=jnp.float32) / head_size
    )
    angles = positions.astype(jnp.float32)[:, None] * frequency[None, :]
    cosine_table = jnp.concatenate([jnp.cos(angles), jnp.cos(angles)], 1)
    sine_table = jnp.concatenate([jnp.sin(angles), jnp.sin(angles)], 1)
    return (cosine_table, sine_table)


def unrotate(gradient, cosine_table, sine_table):
    half_size = gradient.shape[-1] // 2
    scaled = gradient * sine_table
    turned = jnp.concatenate([-scaled[..., half_size:], scaled[..., :half_size]], -1)
    return gradient * cosine_table - turned


def arrange_features(rows, seq_count):
    full_blocks = D // BLOCK
    piece = BLOCK // seq_count
    tail_piece = (D - full_blocks * BLOCK) // seq_count
    count = rows.shape[0]
    main = rows[:, : full_blocks * BLOCK].reshape(count, full_blocks, seq_count, piece)
    main = main.transpose(0, 2, 1, 3).reshape(count, seq_count, full_blocks * piece)
    tail = rows[:, full_blocks * BLOCK :].reshape(count, seq_count, tail_piece)
    return jnp.concatenate([main, tail], 2).reshape(count, D)


def owned_block(arranged, owner_row, block_pick, seq_count):
    full_blocks = D // BLOCK
    piece = BLOCK // seq_count
    tail_piece = (D - full_blocks * BLOCK) // seq_count
    columns = arranged.shape[1]
    core = lax.axis_index("seq") % 2
    paired = arranged.reshape(seq_count // 2, 2, -1, columns)
    kept = lax.dynamic_index_in_dim(paired, core, 1, keepdims=False)
    given = lax.dynamic_index_in_dim(paired, 1 - core, 1, keepdims=False)
    taken = lax.ppermute(given, "seq", [(src, src ^ 1) for src in range(seq_count)])
    summed = (kept.astype(jnp.float32) + taken.astype(jnp.float32)).astype(jnp.bfloat16)
    groups = [list(range(parity, seq_count, 2)) for parity in range(2)]
    mine = lax.psum_scatter(
        summed.reshape(-1, columns), "seq", scatter_dimension=0, tiled=True,
        axis_index_groups=groups,
    )
    mine = jnp.concatenate(
        [mine, jnp.zeros((NBLK * piece - mine.shape[0], columns), mine.dtype)], 0
    ).reshape(NBLK, piece, columns)
    destinations = jnp.arange(seq_count, dtype=jnp.int32)
    dest_block = jnp.sum(
        jnp.where(
            owner_row[None, :] == destinations[:, None],
            jnp.arange(NBLK, dtype=jnp.int32)[None, :],
            0,
        ),
        1,
    )
    send = jnp.take(mine, dest_block, axis=0)
    received = lax.all_to_all(send, "seq", 0, 0, tiled=False)
    main_block = received.reshape(BLOCK, columns)
    tail_block = jnp.concatenate(
        [
            received[:, :tail_piece].reshape(tail_piece * seq_count, columns),
            jnp.zeros((BLOCK - tail_piece * seq_count, columns), received.dtype),
        ],
        0,
    )
    return jnp.where(block_pick == full_blocks, tail_block, main_block)

def per_device(inputs, queries, key_rows, values, out_grad, band_start, owners):
    tok_rows = queries.shape[0]
    seq_count = lax.axis_size("seq")
    seq_index = lax.axis_index("seq")
    group_index = lax.axis_index("head")
    tokens_all = tok_rows * seq_count
    earlier_keys, earlier_values = shifted((key_rows, values), "seq", 1)
    key_all = jnp.concatenate([earlier_keys, key_rows], 0)
    value_all = jnp.concatenate([earlier_values, values], 0)
    band_rel = band_start - (seq_index * tok_rows - WINDOW)
    grad_query, grad_keys, grad_values = attention_backward(
        band_rel, queries, out_grad, key_all, value_all
    )
    grad_keys = grad_keys.reshape(2 * tok_rows, KV_DEV, HD)
    grad_values = grad_values.reshape(2 * tok_rows, KV_DEV, HD)
    rim_keys, rim_values = (
        shifted(grad_keys[:tok_rows].astype(jnp.bfloat16), "seq", -1).astype(jnp.float32),
        shifted(grad_values[:tok_rows].astype(jnp.bfloat16), "seq", -1).astype(jnp.float32),
    )
    own_keys = grad_keys[tok_rows:] + rim_keys
    own_values = grad_values[tok_rows:] + rim_values
    positions = seq_index * tok_rows + jnp.arange(tok_rows, dtype=jnp.int32)
    cosine_table, sine_table = rope_tables(positions, HD)
    query_pre = unrotate(
        grad_query.reshape(tok_rows, KV_DEV * QPK, HD),
        cosine_table[:, None, :],
        sine_table[:, None, :],
    )
    key_pre = unrotate(own_keys, cosine_table[:, None, :], sine_table[:, None, :])
    column_grads = jnp.concatenate(
        [
            query_pre.reshape(tok_rows, KV_DEV * QPK * HD),
            key_pre.reshape(tok_rows, KV_DEV * HD),
            own_values.reshape(tok_rows, KV_DEV * HD),
        ],
        1,
    ).astype(jnp.bfloat16)
    column_count = column_grads.shape[1]
    partial_sum = lax.dot_general(
        lax.all_gather(arrange_features(inputs, seq_count), "head", axis=0, tiled=True),
        column_grads,
        (((0,), (0,)), ((), ())),
        preferred_element_type=jnp.float32,
    )
    owner_row = lax.dynamic_index_in_dim(owners, group_index, 0, keepdims=False)
    is_mine = owner_row == seq_index
    block_pick = jnp.sum(jnp.where(is_mine, jnp.arange(NBLK, dtype=jnp.int32), 0))
    block_part = owned_block(partial_sum.astype(jnp.bfloat16), owner_row, block_pick, seq_count)
    def gram_pair(part_rows):
        left_value = (
            lax.dot_general(
                part_rows, part_rows, (((1,), (1,)), ((), ())), preferred_element_type=jnp.float32
            )
            / tokens_all
        )
        right_value = (
            lax.dot_general(
                part_rows, part_rows, (((0,), (0,)), ((), ())), preferred_element_type=jnp.float32
            )
            / tokens_all
        )
        return (left_value, right_value)

    def nothing(part_rows):
        return (
            jnp.zeros((BLOCK, BLOCK), jnp.float32),
            jnp.zeros((column_count, column_count), jnp.float32),
        )

    left_stat, right_stat = lax.cond(jnp.any(is_mine), gram_pair, nothing, block_part)
    return (left_stat[None, None], right_stat[None, None])


def solution(mesh):
    in_specs = (
        P(("seq", "head"), None),
        P("seq", "head"),
        P("seq", "head"),
        P("seq", "head"),
        P("seq", "head"),
        P("seq"),
        P(),
    )
    out_specs = (P("seq", "head", None, None), P("seq", "head", None, None))
    return jax.shard_map(
        per_device, mesh=mesh, in_specs=in_specs, out_specs=out_specs, check_vma=False
    )
```

```python
import jax
import jax.numpy as jnp
from jax import lax
from jax.sharding import PartitionSpec as P
from jax.experimental import pallas as pl
from jax.experimental.pallas import tpu as pltpu

D = 5376
HD = 128
KV_DEV = 2
QPK = 2
WINDOW = 1024
BLOCK = 1024
NBLK = 6


score_scale = 168.0 ** (-0.5)
rotary_frequency_base = 10000.0
neg_large = -1e30
QBLK = 256


def attention_kernel(band_ref, q_ref, do_ref, k_ref, v_ref, dq_ref, dk_ref, dv_ref):
    tok_rows = q_ref.shape[0]
    span = QBLK + WINDOW
    dk_ref[...] = jnp.zeros(dk_ref.shape, jnp.float32)
    dv_ref[...] = jnp.zeros(dv_ref.shape, jnp.float32)
    def one_block(qb, carry):
        q0 = pl.multiple_of(qb * QBLK, QBLK)
        band = band_ref[pl.ds(q0, QBLK), :]
        band = jnp.concatenate([band, band], 0)
        col = lax.broadcasted_iota(jnp.int32, (QPK * QBLK, span), 1)
        row = lax.broadcasted_iota(jnp.int32, (QPK * QBLK, span), 0) % QBLK
        allowed = (col + q0 >= band) & (col <= row + WINDOW)
        for g in range(KV_DEV):
            base = g * QPK * HD
            qs = jnp.concatenate(
                [q_ref[pl.ds(q0, QBLK), base + r * HD:base + (r + 1) * HD] for r in range(QPK)], 0)
            dos = jnp.concatenate(
                [do_ref[pl.ds(q0, QBLK), base + r * HD:base + (r + 1) * HD] for r in range(QPK)], 0)
            keys = k_ref[pl.ds(q0, span), g * HD:(g + 1) * HD]
            vals = v_ref[pl.ds(q0, span), g * HD:(g + 1) * HD]
            logits = lax.dot_general(qs, keys, (((1,), (1,)), ((), ())),
                                     preferred_element_type=jnp.float32) * score_scale
            masked = jnp.where(allowed, logits, neg_large)
            top = jnp.max(masked, -1, keepdims=True)
            expo = jnp.where(allowed, jnp.exp(masked - top), 0.0)
            attend = expo / jnp.sum(expo, -1, keepdims=True)
            grad_attend = lax.dot_general(dos, vals, (((1,), (1,)), ((), ())),
                                          preferred_element_type=jnp.float32)
            row_dot = jnp.sum(attend * grad_attend, -1, keepdims=True)
            grad_score = (attend * (grad_attend - row_dot) * score_scale).astype(jnp.bfloat16)
            dqs = jnp.dot(grad_score, keys, preferred_element_type=jnp.float32)
            for r in range(QPK):
                dq_ref[pl.ds(q0, QBLK), base + r * HD:base + (r + 1) * HD] = dqs[r * QBLK:(r + 1) * QBLK]
            dk_ref[pl.ds(q0, span), g * HD:(g + 1) * HD] += lax.dot_general(
                grad_score, qs, (((0,), (0,)), ((), ())), preferred_element_type=jnp.float32)
            dv_ref[pl.ds(q0, span), g * HD:(g + 1) * HD] += lax.dot_general(
                attend.astype(jnp.bfloat16), dos, (((0,), (0,)), ((), ())),
                preferred_element_type=jnp.float32)
        return carry

    lax.fori_loop(0, tok_rows // QBLK, one_block, 0)


def attention_backward(band_rel, queries, out_grad, key_all, value_all):
    tok_rows = queries.shape[0]
    vmem = pl.BlockSpec(memory_space=pltpu.VMEM)
    return pl.pallas_call(
        attention_kernel,
        out_shape=(
            jax.ShapeDtypeStruct(queries.shape, jnp.float32),
            jax.ShapeDtypeStruct(key_all.shape, jnp.float32),
            jax.ShapeDtypeStruct(value_all.shape, jnp.float32),
        ),
        in_specs=[vmem] * 5,
        out_specs=(vmem, vmem, vmem),
    )(band_rel.reshape(tok_rows, 1), queries, out_grad, key_all, value_all)


def shifted(value, axis, steps):
    count = lax.axis_size(axis)
    initial, last = (max(0, -steps), min(count, count - steps))
    return lax.ppermute(value, axis, [(source, source + steps) for source in range(initial, last)])


def rope_tables(positions, head_size):
    half_size = head_size // 2
    frequency = jnp.power(
        rotary_frequency_base, -2.0 * jnp.arange(half_size, dtype=jnp.float32) / head_size
    )
    angles = positions.astype(jnp.float32)[:, None] * frequency[None, :]
    cosine_table = jnp.concatenate([jnp.cos(angles), jnp.cos(angles)], 1)
    sine_table = jnp.concatenate([jnp.sin(angles), jnp.sin(angles)], 1)
    return (cosine_table, sine_table)


def unrotate(gradient, cosine_table, sine_table):
    half_size = gradient.shape[-1] // 2
    scaled = gradient * sine_table
    turned = jnp.concatenate([-scaled[..., half_size:], scaled[..., :half_size]], -1)
    return gradient * cosine_table - turned


def arrange_features(rows, seq_count):
    full_blocks = D // BLOCK
    piece = BLOCK // seq_count
    tail_piece = (D - full_blocks * BLOCK) // seq_count
    count = rows.shape[0]
    main = rows[:, : full_blocks * BLOCK].reshape(count, full_blocks, seq_count, piece)
    main = main.transpose(0, 2, 1, 3).reshape(count, seq_count, full_blocks * piece)
    tail = rows[:, full_blocks * BLOCK :].reshape(count, seq_count, tail_piece)
    return jnp.concatenate([main, tail], 2).reshape(count, D)


def owned_block(mine, owner_row, block_pick, seq_count):
    full_blocks = D // BLOCK
    piece = BLOCK // seq_count
    tail_piece = (D - full_blocks * BLOCK) // seq_count
    columns = mine.shape[1]
    mine = jnp.concatenate(
        [mine, jnp.zeros((NBLK * piece - mine.shape[0], columns), mine.dtype)], 0
    ).reshape(NBLK, piece, columns)
    destinations = jnp.arange(seq_count, dtype=jnp.int32)
    dest_block = jnp.sum(
        jnp.where(
            owner_row[None, :] == destinations[:, None],
            jnp.arange(NBLK, dtype=jnp.int32)[None, :],
            0,
        ),
        1,
    )
    send = jnp.take(mine, dest_block, axis=0)
    received = lax.all_to_all(send, "seq", 0, 0, tiled=False)
    main_block = received.reshape(BLOCK, columns)
    tail_block = jnp.concatenate(
        [
            received[:, :tail_piece].reshape(tail_piece * seq_count, columns),
            jnp.zeros((BLOCK - tail_piece * seq_count, columns), received.dtype),
        ],
        0,
    )
    return jnp.where(block_pick == full_blocks, tail_block, main_block)

def per_device(inputs, queries, key_rows, values, out_grad, band_start, owners):
    tok_rows = queries.shape[0]
    seq_count = lax.axis_size("seq")
    seq_index = lax.axis_index("seq")
    group_index = lax.axis_index("head")
    tokens_all = tok_rows * seq_count
    earlier_keys, earlier_values = shifted((key_rows, values), "seq", 1)
    key_all = jnp.concatenate([earlier_keys, key_rows], 0)
    value_all = jnp.concatenate([earlier_values, values], 0)
    band_rel = band_start - (seq_index * tok_rows - WINDOW)
    grad_query, grad_keys, grad_values = attention_backward(
        band_rel, queries, out_grad, key_all, value_all
    )
    grad_keys = grad_keys.reshape(2 * tok_rows, KV_DEV, HD)
    grad_values = grad_values.reshape(2 * tok_rows, KV_DEV, HD)
    rim_keys, rim_values = (
        shifted(grad_keys[:tok_rows].astype(jnp.bfloat16), "seq", -1).astype(jnp.float32),
        shifted(grad_values[:tok_rows].astype(jnp.bfloat16), "seq", -1).astype(jnp.float32),
    )
    own_keys = grad_keys[tok_rows:] + rim_keys
    own_values = grad_values[tok_rows:] + rim_values
    positions = seq_index * tok_rows + jnp.arange(tok_rows, dtype=jnp.int32)
    cosine_table, sine_table = rope_tables(positions, HD)
    query_pre = unrotate(
        grad_query.reshape(tok_rows, KV_DEV * QPK, HD),
        cosine_table[:, None, :],
        sine_table[:, None, :],
    )
    key_pre = unrotate(own_keys, cosine_table[:, None, :], sine_table[:, None, :])
    column_grads = jnp.concatenate(
        [
            query_pre.reshape(tok_rows, KV_DEV * QPK * HD),
            key_pre.reshape(tok_rows, KV_DEV * HD),
            own_values.reshape(tok_rows, KV_DEV * HD),
        ],
        1,
    ).astype(jnp.bfloat16)
    column_count = column_grads.shape[1]
    core = seq_index % 2
    paired = arrange_features(inputs, seq_count).reshape(inputs.shape[0], seq_count // 2, 2, -1)
    local = jnp.concatenate(
        [
            lax.dynamic_index_in_dim(paired, 1 - core, 2, keepdims=False),
            lax.dynamic_index_in_dim(paired, core, 2, keepdims=False),
        ],
        1,
    ).reshape(inputs.shape[0], D)
    gathered = lax.all_gather(local, "head", axis=0, tiled=True)
    half = D // 2
    given = lax.dot_general(
        gathered[:, :half], column_grads, (((0,), (0,)), ((), ())),
        preferred_element_type=jnp.float32,
    ).astype(jnp.bfloat16)
    taken = lax.ppermute(given, "seq", [(src, src ^ 1) for src in range(seq_count)])
    kept = lax.dot_general(
        gathered[:, half:], column_grads, (((0,), (0,)), ((), ())),
        preferred_element_type=jnp.float32,
    ).astype(jnp.bfloat16)
    summed = (kept.astype(jnp.float32) + taken.astype(jnp.float32)).astype(jnp.bfloat16)
    groups = [list(range(parity, seq_count, 2)) for parity in range(2)]
    mine = lax.psum_scatter(
        summed, "seq", scatter_dimension=0, tiled=True, axis_index_groups=groups
    )
    owner_row = lax.dynamic_index_in_dim(owners, group_index, 0, keepdims=False)
    is_mine = owner_row == seq_index
    block_pick = jnp.sum(jnp.where(is_mine, jnp.arange(NBLK, dtype=jnp.int32), 0))
    block_part = owned_block(mine, owner_row, block_pick, seq_count)
    def gram_pair(part_rows):
        left_value = (
            lax.dot_general(
                part_rows, part_rows, (((1,), (1,)), ((), ())), preferred_element_type=jnp.float32
            )
            / tokens_all
        )
        right_value = (
            lax.dot_general(
                part_rows, part_rows, (((0,), (0,)), ((), ())), preferred_element_type=jnp.float32
            )
            / tokens_all
        )
        return (left_value, right_value)

    def nothing(part_rows):
        return (
            jnp.zeros((BLOCK, BLOCK), jnp.float32),
            jnp.zeros((column_count, column_count), jnp.float32),
        )

    left_stat, right_stat = lax.cond(jnp.any(is_mine), gram_pair, nothing, block_part)
    return (left_stat[None, None], right_stat[None, None])


def solution(mesh):
    in_specs = (
        P(("seq", "head"), None),
        P("seq", "head"),
        P("seq", "head"),
        P("seq", "head"),
        P("seq", "head"),
        P("seq"),
        P(),
    )
    out_specs = (P("seq", "head", None, None), P("seq", "head", None, None))
    return jax.shard_map(
        per_device, mesh=mesh, in_specs=in_specs, out_specs=out_specs, check_vma=False
    )
```

```python
import jax
import jax.numpy as jnp
from jax import lax
from jax.sharding import PartitionSpec as P
from jax.experimental import pallas as pl
from jax.experimental.pallas import tpu as pltpu

D = 5376
HD = 128
KV_DEV = 2
QPK = 2
WINDOW = 1024
BLOCK = 1024
NBLK = 6


score_scale = 168.0 ** (-0.5)
rotary_frequency_base = 10000.0
neg_large = -1e30
QBLK = 256


def attention_kernel(band_ref, q_ref, do_ref, k_ref, v_ref, dq_ref, dk_ref, dv_ref):
    tok_rows = q_ref.shape[0]
    span = QBLK + WINDOW
    dk_ref[...] = jnp.zeros(dk_ref.shape, jnp.float32)
    dv_ref[...] = jnp.zeros(dv_ref.shape, jnp.float32)
    def one_block(qb, carry):
        q0 = pl.multiple_of(qb * QBLK, QBLK)
        band = band_ref[pl.ds(q0, QBLK), :]
        band = jnp.concatenate([band, band], 0)
        col = lax.broadcasted_iota(jnp.int32, (QPK * QBLK, span), 1)
        row = lax.broadcasted_iota(jnp.int32, (QPK * QBLK, span), 0) % QBLK
        allowed = (col + q0 >= band) & (col <= row + WINDOW)
        for g in range(KV_DEV):
            base = g * QPK * HD
            qs = jnp.concatenate(
                [q_ref[pl.ds(q0, QBLK), base + r * HD:base + (r + 1) * HD] for r in range(QPK)], 0)
            dos = jnp.concatenate(
                [do_ref[pl.ds(q0, QBLK), base + r * HD:base + (r + 1) * HD] for r in range(QPK)], 0)
            keys = k_ref[pl.ds(q0, span), g * HD:(g + 1) * HD]
            vals = v_ref[pl.ds(q0, span), g * HD:(g + 1) * HD]
            logits = lax.dot_general(qs, keys, (((1,), (1,)), ((), ())),
                                     preferred_element_type=jnp.float32) * score_scale
            masked = jnp.where(allowed, logits, neg_large)
            top = jnp.max(masked, -1, keepdims=True)
            expo = jnp.where(allowed, jnp.exp(masked - top), 0.0)
            attend = expo / jnp.sum(expo, -1, keepdims=True)
            grad_attend = lax.dot_general(dos, vals, (((1,), (1,)), ((), ())),
                                          preferred_element_type=jnp.float32)
            row_dot = jnp.sum(attend * grad_attend, -1, keepdims=True)
            grad_score = (attend * (grad_attend - row_dot) * score_scale).astype(jnp.bfloat16)
            dqs = jnp.dot(grad_score, keys, preferred_element_type=jnp.float32)
            for r in range(QPK):
                dq_ref[pl.ds(q0, QBLK), base + r * HD:base + (r + 1) * HD] = dqs[r * QBLK:(r + 1) * QBLK]
            dk_ref[pl.ds(q0, span), g * HD:(g + 1) * HD] += lax.dot_general(
                grad_score, qs, (((0,), (0,)), ((), ())), preferred_element_type=jnp.float32)
            dv_ref[pl.ds(q0, span), g * HD:(g + 1) * HD] += lax.dot_general(
                attend.astype(jnp.bfloat16), dos, (((0,), (0,)), ((), ())),
                preferred_element_type=jnp.float32)
        return carry

    lax.fori_loop(0, tok_rows // QBLK, one_block, 0)


def attention_backward(band_rel, queries, out_grad, key_all, value_all):
    tok_rows = queries.shape[0]
    vmem = pl.BlockSpec(memory_space=pltpu.VMEM)
    return pl.pallas_call(
        attention_kernel,
        out_shape=(
            jax.ShapeDtypeStruct(queries.shape, jnp.float32),
            jax.ShapeDtypeStruct(key_all.shape, jnp.float32),
            jax.ShapeDtypeStruct(value_all.shape, jnp.float32),
        ),
        in_specs=[vmem] * 5,
        out_specs=(vmem, vmem, vmem),
    )(band_rel.reshape(tok_rows, 1), queries, out_grad, key_all, value_all)


def shifted(value, axis, steps):
    count = lax.axis_size(axis)
    initial, last = (max(0, -steps), min(count, count - steps))
    return lax.ppermute(value, axis, [(source, source + steps) for source in range(initial, last)])


def rope_tables(positions, head_size):
    half_size = head_size // 2
    frequency = jnp.power(
        rotary_frequency_base, -2.0 * jnp.arange(half_size, dtype=jnp.float32) / head_size
    )
    angles = positions.astype(jnp.float32)[:, None] * frequency[None, :]
    cosine_table = jnp.concatenate([jnp.cos(angles), jnp.cos(angles)], 1)
    sine_table = jnp.concatenate([jnp.sin(angles), jnp.sin(angles)], 1)
    return (cosine_table, sine_table)


def unrotate(gradient, cosine_table, sine_table):
    half_size = gradient.shape[-1] // 2
    scaled = gradient * sine_table
    turned = jnp.concatenate([-scaled[..., half_size:], scaled[..., :half_size]], -1)
    return gradient * cosine_table - turned


def arrange_features(rows, seq_count):
    full_blocks = D // BLOCK
    piece = BLOCK // seq_count
    tail_piece = (D - full_blocks * BLOCK) // seq_count
    count = rows.shape[0]
    main = rows[:, : full_blocks * BLOCK].reshape(count, full_blocks, seq_count, piece)
    main = main.transpose(0, 2, 1, 3).reshape(count, seq_count, full_blocks * piece)
    tail = rows[:, full_blocks * BLOCK :].reshape(count, seq_count, tail_piece)
    return jnp.concatenate([main, tail], 2).reshape(count, D)


def owned_block(mine, owner_row, block_pick, seq_count):
    full_blocks = D // BLOCK
    piece = BLOCK // seq_count
    tail_piece = (D - full_blocks * BLOCK) // seq_count
    columns = mine.shape[1]
    mine = jnp.concatenate(
        [mine, jnp.zeros((NBLK * piece - mine.shape[0], columns), mine.dtype)], 0
    ).reshape(NBLK, piece, columns)
    destinations = jnp.arange(seq_count, dtype=jnp.int32)
    dest_block = jnp.sum(
        jnp.where(
            owner_row[None, :] == destinations[:, None],
            jnp.arange(NBLK, dtype=jnp.int32)[None, :],
            0,
        ),
        1,
    )
    send = jnp.take(mine, dest_block, axis=0)
    received = lax.all_to_all(send, "seq", 0, 0, tiled=False)
    main_block = received.reshape(BLOCK, columns)
    tail_block = jnp.concatenate(
        [
            received[:, :tail_piece].reshape(tail_piece * seq_count, columns),
            jnp.zeros((BLOCK - tail_piece * seq_count, columns), received.dtype),
        ],
        0,
    )
    return jnp.where(block_pick == full_blocks, tail_block, main_block)

def per_device(inputs, queries, key_rows, values, out_grad, band_start, owners):
    tok_rows = queries.shape[0]
    seq_count = lax.axis_size("seq")
    seq_index = lax.axis_index("seq")
    group_index = lax.axis_index("head")
    tokens_all = tok_rows * seq_count
    earlier_keys, earlier_values = shifted((key_rows, values), "seq", 1)
    key_all = jnp.concatenate([earlier_keys, key_rows], 0)
    value_all = jnp.concatenate([earlier_values, values], 0)
    band_rel = band_start - (seq_index * tok_rows - WINDOW)
    grad_query, grad_keys, grad_values = attention_backward(
        band_rel, queries, out_grad, key_all, value_all
    )
    grad_keys = grad_keys.reshape(2 * tok_rows, KV_DEV, HD)
    grad_values = grad_values.reshape(2 * tok_rows, KV_DEV, HD)
    rim_keys, rim_values = (
        shifted(grad_keys[:tok_rows].astype(jnp.bfloat16), "seq", -1).astype(jnp.float32),
        shifted(grad_values[:tok_rows].astype(jnp.bfloat16), "seq", -1).astype(jnp.float32),
    )
    own_keys = grad_keys[tok_rows:] + rim_keys
    own_values = grad_values[tok_rows:] + rim_values
    positions = seq_index * tok_rows + jnp.arange(tok_rows, dtype=jnp.int32)
    cosine_table, sine_table = rope_tables(positions, HD)
    query_pre = unrotate(
        grad_query.reshape(tok_rows, KV_DEV * QPK, HD),
        cosine_table[:, None, :],
        sine_table[:, None, :],
    )
    key_pre = unrotate(own_keys, cosine_table[:, None, :], sine_table[:, None, :])
    column_grads = jnp.concatenate(
        [
            query_pre.reshape(tok_rows, KV_DEV * QPK * HD),
            key_pre.reshape(tok_rows, KV_DEV * HD),
            own_values.reshape(tok_rows, KV_DEV * HD),
        ],
        1,
    ).astype(jnp.bfloat16)
    column_count = column_grads.shape[1]
    core = seq_index % 2
    paired = arrange_features(inputs, seq_count).reshape(inputs.shape[0], seq_count // 2, 2, -1)
    local = jnp.concatenate(
        [
            lax.dynamic_index_in_dim(paired, 1 - core, 2, keepdims=False),
            lax.dynamic_index_in_dim(paired, core, 2, keepdims=False),
        ],
        1,
    ).reshape(inputs.shape[0], D)
    gathered = lax.all_gather(local, "head", axis=0, tiled=True)
    half = D // 2
    given = lax.dot_general(
        gathered[:, :half], column_grads, (((0,), (0,)), ((), ())),
        preferred_element_type=jnp.float32,
    ).astype(jnp.bfloat16)
    taken = lax.ppermute(given, "seq", [(src, src ^ 1) for src in range(seq_count)])
    kept = lax.dot_general(
        gathered[:, half:], column_grads, (((0,), (0,)), ((), ())),
        preferred_element_type=jnp.float32,
    ).astype(jnp.bfloat16)
    kept, taken = lax.optimization_barrier((kept, taken))
    summed = (kept.astype(jnp.float32) + taken.astype(jnp.float32)).astype(jnp.bfloat16)
    groups = [list(range(parity, seq_count, 2)) for parity in range(2)]
    mine = lax.psum_scatter(
        summed, "seq", scatter_dimension=0, tiled=True, axis_index_groups=groups
    )
    owner_row = lax.dynamic_index_in_dim(owners, group_index, 0, keepdims=False)
    is_mine = owner_row == seq_index
    block_pick = jnp.sum(jnp.where(is_mine, jnp.arange(NBLK, dtype=jnp.int32), 0))
    block_part = owned_block(mine, owner_row, block_pick, seq_count)
    def gram_pair(part_rows):
        left_value = (
            lax.dot_general(
                part_rows, part_rows, (((1,), (1,)), ((), ())), preferred_element_type=jnp.float32
            )
            / tokens_all
        )
        right_value = (
            lax.dot_general(
                part_rows, part_rows, (((0,), (0,)), ((), ())), preferred_element_type=jnp.float32
            )
            / tokens_all
        )
        return (left_value, right_value)

    def nothing(part_rows):
        return (
            jnp.zeros((BLOCK, BLOCK), jnp.float32),
            jnp.zeros((column_count, column_count), jnp.float32),
        )

    left_stat, right_stat = lax.cond(jnp.any(is_mine), gram_pair, nothing, block_part)
    return (left_stat[None, None], right_stat[None, None])


def solution(mesh):
    in_specs = (
        P(("seq", "head"), None),
        P("seq", "head"),
        P("seq", "head"),
        P("seq", "head"),
        P("seq", "head"),
        P("seq"),
        P(),
    )
    out_specs = (P("seq", "head", None, None), P("seq", "head", None, None))
    return jax.shard_map(
        per_device, mesh=mesh, in_specs=in_specs, out_specs=out_specs, check_vma=False
    )
```

```python
import jax
import jax.numpy as jnp
from jax import lax
from jax.sharding import PartitionSpec as P
from jax.experimental import pallas as pl
from jax.experimental.pallas import tpu as pltpu

D = 5376
HD = 128
KV_DEV = 2
QPK = 2
WINDOW = 1024
BLOCK = 1024
NBLK = 6


score_scale = 168.0 ** (-0.5)
rotary_frequency_base = 10000.0
neg_large = -1e30
QBLK = 256


def attention_kernel(band_ref, q_ref, do_ref, k_ref, v_ref, dq_ref, dk_ref, dv_ref):
    tok_rows = q_ref.shape[0]
    span = QBLK + WINDOW
    dk_ref[...] = jnp.zeros(dk_ref.shape, jnp.float32)
    dv_ref[...] = jnp.zeros(dv_ref.shape, jnp.float32)
    def one_block(qb, carry):
        q0 = pl.multiple_of(qb * QBLK, QBLK)
        band = band_ref[pl.ds(q0, QBLK), :]
        band = jnp.concatenate([band, band], 0)
        col = lax.broadcasted_iota(jnp.int32, (QPK * QBLK, span), 1)
        row = lax.broadcasted_iota(jnp.int32, (QPK * QBLK, span), 0) % QBLK
        allowed = (col + q0 >= band) & (col <= row + WINDOW)
        for g in range(KV_DEV):
            base = g * QPK * HD
            qs = jnp.concatenate(
                [q_ref[pl.ds(q0, QBLK), base + r * HD:base + (r + 1) * HD] for r in range(QPK)], 0)
            dos = jnp.concatenate(
                [do_ref[pl.ds(q0, QBLK), base + r * HD:base + (r + 1) * HD] for r in range(QPK)], 0)
            keys = k_ref[pl.ds(q0, span), g * HD:(g + 1) * HD]
            vals = v_ref[pl.ds(q0, span), g * HD:(g + 1) * HD]
            logits = lax.dot_general(qs, keys, (((1,), (1,)), ((), ())),
                                     preferred_element_type=jnp.float32) * score_scale
            masked = jnp.where(allowed, logits, neg_large)
            top = jnp.max(masked, -1, keepdims=True)
            expo = jnp.where(allowed, jnp.exp(masked - top), 0.0)
            attend = expo / jnp.sum(expo, -1, keepdims=True)
            grad_attend = lax.dot_general(dos, vals, (((1,), (1,)), ((), ())),
                                          preferred_element_type=jnp.float32)
            row_dot = jnp.sum(attend * grad_attend, -1, keepdims=True)
            grad_score = (attend * (grad_attend - row_dot) * score_scale).astype(jnp.bfloat16)
            dqs = jnp.dot(grad_score, keys, preferred_element_type=jnp.float32)
            for r in range(QPK):
                dq_ref[pl.ds(q0, QBLK), base + r * HD:base + (r + 1) * HD] = dqs[r * QBLK:(r + 1) * QBLK]
            dk_ref[pl.ds(q0, span), g * HD:(g + 1) * HD] += lax.dot_general(
                grad_score, qs, (((0,), (0,)), ((), ())), preferred_element_type=jnp.float32)
            dv_ref[pl.ds(q0, span), g * HD:(g + 1) * HD] += lax.dot_general(
                attend.astype(jnp.bfloat16), dos, (((0,), (0,)), ((), ())),
                preferred_element_type=jnp.float32)
        return carry

    lax.fori_loop(0, tok_rows // QBLK, one_block, 0)


def attention_backward(band_rel, queries, out_grad, key_all, value_all):
    tok_rows = queries.shape[0]
    vmem = pl.BlockSpec(memory_space=pltpu.VMEM)
    return pl.pallas_call(
        attention_kernel,
        out_shape=(
            jax.ShapeDtypeStruct(queries.shape, jnp.float32),
            jax.ShapeDtypeStruct(key_all.shape, jnp.float32),
            jax.ShapeDtypeStruct(value_all.shape, jnp.float32),
        ),
        in_specs=[vmem] * 5,
        out_specs=(vmem, vmem, vmem),
    )(band_rel.reshape(tok_rows, 1), queries, out_grad, key_all, value_all)


def shifted(value, axis, steps):
    count = lax.axis_size(axis)
    initial, last = (max(0, -steps), min(count, count - steps))
    return lax.ppermute(value, axis, [(source, source + steps) for source in range(initial, last)])


def rope_tables(positions, head_size):
    half_size = head_size // 2
    frequency = jnp.power(
        rotary_frequency_base, -2.0 * jnp.arange(half_size, dtype=jnp.float32) / head_size
    )
    angles = positions.astype(jnp.float32)[:, None] * frequency[None, :]
    cosine_table = jnp.concatenate([jnp.cos(angles), jnp.cos(angles)], 1)
    sine_table = jnp.concatenate([jnp.sin(angles), jnp.sin(angles)], 1)
    return (cosine_table, sine_table)


def unrotate(gradient, cosine_table, sine_table):
    half_size = gradient.shape[-1] // 2
    scaled = gradient * sine_table
    turned = jnp.concatenate([-scaled[..., half_size:], scaled[..., :half_size]], -1)
    return gradient * cosine_table - turned


def arrange_features(rows, seq_count):
    full_blocks = D // BLOCK
    piece = BLOCK // seq_count
    tail_piece = (D - full_blocks * BLOCK) // seq_count
    count = rows.shape[0]
    main = rows[:, : full_blocks * BLOCK].reshape(count, full_blocks, seq_count, piece)
    main = main.transpose(0, 2, 1, 3).reshape(count, seq_count, full_blocks * piece)
    tail = rows[:, full_blocks * BLOCK :].reshape(count, seq_count, tail_piece)
    return jnp.concatenate([main, tail], 2).reshape(count, D)


def owned_block(mine, owner_row, block_pick, seq_count):
    full_blocks = D // BLOCK
    piece = BLOCK // seq_count
    tail_piece = (D - full_blocks * BLOCK) // seq_count
    columns = mine.shape[1]
    mine = jnp.concatenate(
        [mine, jnp.zeros((NBLK * piece - mine.shape[0], columns), mine.dtype)], 0
    ).reshape(NBLK, piece, columns)
    destinations = jnp.arange(seq_count, dtype=jnp.int32)
    dest_block = jnp.sum(
        jnp.where(
            owner_row[None, :] == destinations[:, None],
            jnp.arange(NBLK, dtype=jnp.int32)[None, :],
            0,
        ),
        1,
    )
    send = jnp.take(mine, dest_block, axis=0)
    received = lax.all_to_all(send, "seq", 0, 0, tiled=False)
    main_block = received.reshape(BLOCK, columns)
    tail_block = jnp.concatenate(
        [
            received[:, :tail_piece].reshape(tail_piece * seq_count, columns),
            jnp.zeros((BLOCK - tail_piece * seq_count, columns), received.dtype),
        ],
        0,
    )
    return jnp.where(block_pick == full_blocks, tail_block, main_block)

def per_device(inputs, queries, key_rows, values, out_grad, band_start, owners):
    tok_rows = queries.shape[0]
    seq_count = lax.axis_size("seq")
    seq_index = lax.axis_index("seq")
    group_index = lax.axis_index("head")
    tokens_all = tok_rows * seq_count
    earlier_keys, earlier_values = shifted((key_rows, values), "seq", 1)
    key_all = jnp.concatenate([earlier_keys, key_rows], 0)
    value_all = jnp.concatenate([earlier_values, values], 0)
    band_rel = band_start - (seq_index * tok_rows - WINDOW)
    grad_query, grad_keys, grad_values = attention_backward(
        band_rel, queries, out_grad, key_all, value_all
    )
    grad_keys = grad_keys.reshape(2 * tok_rows, KV_DEV, HD)
    grad_values = grad_values.reshape(2 * tok_rows, KV_DEV, HD)
    rim_keys, rim_values = (
        shifted(grad_keys[:tok_rows].astype(jnp.bfloat16), "seq", -1).astype(jnp.float32),
        shifted(grad_values[:tok_rows].astype(jnp.bfloat16), "seq", -1).astype(jnp.float32),
    )
    own_keys = grad_keys[tok_rows:] + rim_keys
    own_values = grad_values[tok_rows:] + rim_values
    positions = seq_index * tok_rows + jnp.arange(tok_rows, dtype=jnp.int32)
    cosine_table, sine_table = rope_tables(positions, HD)
    query_pre = unrotate(
        grad_query.reshape(tok_rows, KV_DEV * QPK, HD),
        cosine_table[:, None, :],
        sine_table[:, None, :],
    )
    key_pre = unrotate(own_keys, cosine_table[:, None, :], sine_table[:, None, :])
    column_grads = jnp.concatenate(
        [
            query_pre.reshape(tok_rows, KV_DEV * QPK * HD),
            key_pre.reshape(tok_rows, KV_DEV * HD),
            own_values.reshape(tok_rows, KV_DEV * HD),
        ],
        1,
    ).astype(jnp.bfloat16)
    column_count = column_grads.shape[1]
    core = seq_index % 2
    paired = arrange_features(inputs, seq_count).reshape(inputs.shape[0], seq_count // 2, 2, -1)
    local = jnp.concatenate(
        [
            lax.dynamic_index_in_dim(paired, 1 - core, 2, keepdims=False),
            lax.dynamic_index_in_dim(paired, core, 2, keepdims=False),
        ],
        1,
    ).reshape(inputs.shape[0], D)
    head_count = lax.axis_size("head")
    lane_count = head_count // 2
    partner = lax.ppermute(
        local, "head", [(src, (src + lane_count) % head_count) for src in range(head_count)]
    )
    upper = group_index // lane_count
    pair = jnp.where(upper == 0, jnp.stack([local, partner]), jnp.stack([partner, local]))
    lanes = [list(range(start, start + lane_count)) for start in (0, lane_count)]
    gathered = lax.all_gather(pair, "head", axis=0, tiled=False, axis_index_groups=lanes)
    gathered = gathered.reshape(-1, D)
    column_grads = (
        column_grads.reshape(2, lane_count, inputs.shape[0], -1)
        .transpose(1, 0, 2, 3)
        .reshape(column_grads.shape)
    )
    half = D // 2
    given = lax.dot_general(
        gathered[:, :half], column_grads, (((0,), (0,)), ((), ())),
        preferred_element_type=jnp.float32,
    ).astype(jnp.bfloat16)
    taken = lax.ppermute(given, "seq", [(src, src ^ 1) for src in range(seq_count)])
    kept = lax.dot_general(
        gathered[:, half:], column_grads, (((0,), (0,)), ((), ())),
        preferred_element_type=jnp.float32,
    ).astype(jnp.bfloat16)
    kept, taken = lax.optimization_barrier((kept, taken))
    summed = (kept.astype(jnp.float32) + taken.astype(jnp.float32)).astype(jnp.bfloat16)
    groups = [list(range(parity, seq_count, 2)) for parity in range(2)]
    mine = lax.psum_scatter(
        summed, "seq", scatter_dimension=0, tiled=True, axis_index_groups=groups
    )
    owner_row = lax.dynamic_index_in_dim(owners, group_index, 0, keepdims=False)
    is_mine = owner_row == seq_index
    block_pick = jnp.sum(jnp.where(is_mine, jnp.arange(NBLK, dtype=jnp.int32), 0))
    block_part = owned_block(mine, owner_row, block_pick, seq_count)
    def gram_pair(part_rows):
        left_value = (
            lax.dot_general(
                part_rows, part_rows, (((1,), (1,)), ((), ())), preferred_element_type=jnp.float32
            )
            / tokens_all
        )
        right_value = (
            lax.dot_general(
                part_rows, part_rows, (((0,), (0,)), ((), ())), preferred_element_type=jnp.float32
            )
            / tokens_all
        )
        return (left_value, right_value)

    def nothing(part_rows):
        return (
            jnp.zeros((BLOCK, BLOCK), jnp.float32),
            jnp.zeros((column_count, column_count), jnp.float32),
        )

    left_stat, right_stat = lax.cond(jnp.any(is_mine), gram_pair, nothing, block_part)
    return (left_stat[None, None], right_stat[None, None])


def solution(mesh):
    in_specs = (
        P(("seq", "head"), None),
        P("seq", "head"),
        P("seq", "head"),
        P("seq", "head"),
        P("seq", "head"),
        P("seq"),
        P(),
    )
    out_specs = (P("seq", "head", None, None), P("seq", "head", None, None))
    return jax.shard_map(
        per_device, mesh=mesh, in_specs=in_specs, out_specs=out_specs, check_vma=False
    )
```

```python
import jax
import jax.numpy as jnp
from jax import lax
from jax.sharding import PartitionSpec as P
from jax.experimental import pallas as pl
from jax.experimental.pallas import tpu as pltpu

D = 5376
HD = 128
KV_DEV = 2
QPK = 2
WINDOW = 1024
BLOCK = 1024
NBLK = 6


score_scale = 168.0 ** (-0.5)
rotary_frequency_base = 10000.0
neg_large = -1e30
QBLK = 256


def attention_kernel(band_ref, q_ref, do_ref, k_ref, v_ref, dq_ref, dk_ref, dv_ref):
    tok_rows = q_ref.shape[0]
    span = QBLK + WINDOW
    dk_ref[...] = jnp.zeros(dk_ref.shape, jnp.float32)
    dv_ref[...] = jnp.zeros(dv_ref.shape, jnp.float32)
    def one_block(qb, carry):
        q0 = pl.multiple_of(qb * QBLK, QBLK)
        band = band_ref[pl.ds(q0, QBLK), :]
        band = jnp.concatenate([band, band], 0)
        col = lax.broadcasted_iota(jnp.int32, (QPK * QBLK, span), 1)
        row = lax.broadcasted_iota(jnp.int32, (QPK * QBLK, span), 0) % QBLK
        allowed = (col + q0 >= band) & (col <= row + WINDOW)
        for g in range(KV_DEV):
            base = g * QPK * HD
            qs = jnp.concatenate(
                [q_ref[pl.ds(q0, QBLK), base + r * HD:base + (r + 1) * HD] for r in range(QPK)], 0)
            dos = jnp.concatenate(
                [do_ref[pl.ds(q0, QBLK), base + r * HD:base + (r + 1) * HD] for r in range(QPK)], 0)
            keys = k_ref[pl.ds(q0, span), g * HD:(g + 1) * HD]
            vals = v_ref[pl.ds(q0, span), g * HD:(g + 1) * HD]
            logits = lax.dot_general(qs, keys, (((1,), (1,)), ((), ())),
                                     preferred_element_type=jnp.float32) * score_scale
            masked = jnp.where(allowed, logits, neg_large)
            top = jnp.max(masked, -1, keepdims=True)
            expo = jnp.where(allowed, jnp.exp(masked - top), 0.0)
            attend = expo / jnp.sum(expo, -1, keepdims=True)
            grad_attend = lax.dot_general(dos, vals, (((1,), (1,)), ((), ())),
                                          preferred_element_type=jnp.float32)
            row_dot = jnp.sum(attend * grad_attend, -1, keepdims=True)
            grad_score = (attend * (grad_attend - row_dot) * score_scale).astype(jnp.bfloat16)
            dqs = jnp.dot(grad_score, keys, preferred_element_type=jnp.float32)
            for r in range(QPK):
                dq_ref[pl.ds(q0, QBLK), base + r * HD:base + (r + 1) * HD] = dqs[r * QBLK:(r + 1) * QBLK]
            dk_ref[pl.ds(q0, span), g * HD:(g + 1) * HD] += lax.dot_general(
                grad_score, qs, (((0,), (0,)), ((), ())), preferred_element_type=jnp.float32)
            dv_ref[pl.ds(q0, span), g * HD:(g + 1) * HD] += lax.dot_general(
                attend.astype(jnp.bfloat16), dos, (((0,), (0,)), ((), ())),
                preferred_element_type=jnp.float32)
        return carry

    lax.fori_loop(0, tok_rows // QBLK, one_block, 0)


def attention_backward(band_rel, queries, out_grad, key_all, value_all):
    tok_rows = queries.shape[0]
    vmem = pl.BlockSpec(memory_space=pltpu.VMEM)
    return pl.pallas_call(
        attention_kernel,
        out_shape=(
            jax.ShapeDtypeStruct(queries.shape, jnp.float32),
            jax.ShapeDtypeStruct(key_all.shape, jnp.float32),
            jax.ShapeDtypeStruct(value_all.shape, jnp.float32),
        ),
        in_specs=[vmem] * 5,
        out_specs=(vmem, vmem, vmem),
    )(band_rel.reshape(tok_rows, 1), queries, out_grad, key_all, value_all)


def shifted(value, axis, steps):
    count = lax.axis_size(axis)
    initial, last = (max(0, -steps), min(count, count - steps))
    return lax.ppermute(value, axis, [(source, source + steps) for source in range(initial, last)])


def rope_tables(positions, head_size):
    half_size = head_size // 2
    frequency = jnp.power(
        rotary_frequency_base, -2.0 * jnp.arange(half_size, dtype=jnp.float32) / head_size
    )
    angles = positions.astype(jnp.float32)[:, None] * frequency[None, :]
    cosine_table = jnp.concatenate([jnp.cos(angles), jnp.cos(angles)], 1)
    sine_table = jnp.concatenate([jnp.sin(angles), jnp.sin(angles)], 1)
    return (cosine_table, sine_table)


def unrotate(gradient, cosine_table, sine_table):
    half_size = gradient.shape[-1] // 2
    scaled = gradient * sine_table
    turned = jnp.concatenate([-scaled[..., half_size:], scaled[..., :half_size]], -1)
    return gradient * cosine_table - turned


def arrange_features(rows, seq_count):
    full_blocks = D // BLOCK
    piece = BLOCK // seq_count
    tail_piece = (D - full_blocks * BLOCK) // seq_count
    count = rows.shape[0]
    main = rows[:, : full_blocks * BLOCK].reshape(count, full_blocks, seq_count, piece)
    main = main.transpose(0, 2, 1, 3).reshape(count, seq_count, full_blocks * piece)
    tail = rows[:, full_blocks * BLOCK :].reshape(count, seq_count, tail_piece)
    return jnp.concatenate([main, tail], 2).reshape(count, D)


def owned_block(mine, owner_row, block_pick, seq_count):
    full_blocks = D // BLOCK
    piece = BLOCK // seq_count
    tail_piece = (D - full_blocks * BLOCK) // seq_count
    columns = mine.shape[1]
    mine = jnp.concatenate(
        [mine, jnp.zeros((NBLK * piece - mine.shape[0], columns), mine.dtype)], 0
    ).reshape(NBLK, piece, columns)
    destinations = jnp.arange(seq_count, dtype=jnp.int32)
    dest_block = jnp.sum(
        jnp.where(
            owner_row[None, :] == destinations[:, None],
            jnp.arange(NBLK, dtype=jnp.int32)[None, :],
            0,
        ),
        1,
    )
    send = jnp.take(mine, dest_block, axis=0)
    received = lax.all_to_all(send, "seq", 0, 0, tiled=False)
    main_block = received.reshape(BLOCK, columns)
    tail_block = jnp.concatenate(
        [
            received[:, :tail_piece].reshape(tail_piece * seq_count, columns),
            jnp.zeros((BLOCK - tail_piece * seq_count, columns), received.dtype),
        ],
        0,
    )
    return jnp.where(block_pick == full_blocks, tail_block, main_block)

def per_device(inputs, queries, key_rows, values, out_grad, band_start, owners):
    tok_rows = queries.shape[0]
    seq_count = lax.axis_size("seq")
    seq_index = lax.axis_index("seq")
    group_index = lax.axis_index("head")
    tokens_all = tok_rows * seq_count
    earlier_keys, earlier_values = shifted((key_rows, values), "seq", 1)
    key_all = jnp.concatenate([earlier_keys, key_rows], 0)
    value_all = jnp.concatenate([earlier_values, values], 0)
    band_rel = band_start - (seq_index * tok_rows - WINDOW)
    grad_query, grad_keys, grad_values = attention_backward(
        band_rel, queries, out_grad, key_all, value_all
    )
    grad_keys = grad_keys.reshape(2 * tok_rows, KV_DEV, HD)
    grad_values = grad_values.reshape(2 * tok_rows, KV_DEV, HD)
    rim_keys, rim_values = (
        shifted(grad_keys[:tok_rows].astype(jnp.bfloat16), "seq", -1).astype(jnp.float32),
        shifted(grad_values[:tok_rows].astype(jnp.bfloat16), "seq", -1).astype(jnp.float32),
    )
    own_keys = grad_keys[tok_rows:] + rim_keys
    own_values = grad_values[tok_rows:] + rim_values
    positions = seq_index * tok_rows + jnp.arange(tok_rows, dtype=jnp.int32)
    cosine_table, sine_table = rope_tables(positions, HD)
    query_pre = unrotate(
        grad_query.reshape(tok_rows, KV_DEV * QPK, HD),
        cosine_table[:, None, :],
        sine_table[:, None, :],
    )
    key_pre = unrotate(own_keys, cosine_table[:, None, :], sine_table[:, None, :])
    column_grads = jnp.concatenate(
        [
            query_pre.reshape(tok_rows, KV_DEV * QPK * HD),
            key_pre.reshape(tok_rows, KV_DEV * HD),
            own_values.reshape(tok_rows, KV_DEV * HD),
        ],
        1,
    ).astype(jnp.bfloat16)
    column_count = column_grads.shape[1]
    core = seq_index % 2
    paired = arrange_features(inputs, seq_count).reshape(inputs.shape[0], seq_count // 2, 2, -1)
    local = jnp.concatenate(
        [
            lax.dynamic_index_in_dim(paired, 1 - core, 2, keepdims=False),
            lax.dynamic_index_in_dim(paired, core, 2, keepdims=False),
        ],
        1,
    ).reshape(inputs.shape[0], D)
    head_count = lax.axis_size("head")
    lane_count = head_count // 2
    partner = lax.ppermute(
        local, "head", [(src, (src + lane_count) % head_count) for src in range(head_count)]
    )
    upper = group_index // lane_count
    pair = jnp.where(upper == 0, jnp.stack([local, partner]), jnp.stack([partner, local]))
    lane = group_index % lane_count

    def from_lane(step):
        return lax.ppermute(
            pair,
            "head",
            [
                (src, (src // lane_count) * lane_count + (src - step) % lane_count)
                for src in range(head_count)
            ],
        )

    gathered = jnp.stack([pair] + [from_lane(step) for step in range(1, lane_count)])
    gathered = gathered.reshape(-1, D)
    lane_grads = column_grads.reshape(2, lane_count, inputs.shape[0], -1)
    lane_grads = jnp.concatenate([lane_grads, lane_grads], 1)
    lane_grads = lax.dynamic_slice_in_dim(lane_grads, lane, lane_count, 1)
    column_grads = lane_grads.transpose(1, 0, 2, 3).reshape(column_grads.shape)
    half = D // 2
    given = lax.dot_general(
        gathered[:, :half], column_grads, (((0,), (0,)), ((), ())),
        preferred_element_type=jnp.float32,
    ).astype(jnp.bfloat16)
    taken = lax.ppermute(given, "seq", [(src, src ^ 1) for src in range(seq_count)])
    kept = lax.dot_general(
        gathered[:, half:], column_grads, (((0,), (0,)), ((), ())),
        preferred_element_type=jnp.float32,
    ).astype(jnp.bfloat16)
    kept, taken = lax.optimization_barrier((kept, taken))
    summed = (kept.astype(jnp.float32) + taken.astype(jnp.float32)).astype(jnp.bfloat16)
    groups = [list(range(parity, seq_count, 2)) for parity in range(2)]
    mine = lax.psum_scatter(
        summed, "seq", scatter_dimension=0, tiled=True, axis_index_groups=groups
    )
    owner_row = lax.dynamic_index_in_dim(owners, group_index, 0, keepdims=False)
    is_mine = owner_row == seq_index
    block_pick = jnp.sum(jnp.where(is_mine, jnp.arange(NBLK, dtype=jnp.int32), 0))
    block_part = owned_block(mine, owner_row, block_pick, seq_count)
    def gram_pair(part_rows):
        left_value = (
            lax.dot_general(
                part_rows, part_rows, (((1,), (1,)), ((), ())), preferred_element_type=jnp.float32
            )
            / tokens_all
        )
        right_value = (
            lax.dot_general(
                part_rows, part_rows, (((0,), (0,)), ((), ())), preferred_element_type=jnp.float32
            )
            / tokens_all
        )
        return (left_value, right_value)

    def nothing(part_rows):
        return (
            jnp.zeros((BLOCK, BLOCK), jnp.float32),
            jnp.zeros((column_count, column_count), jnp.float32),
        )

    left_stat, right_stat = lax.cond(jnp.any(is_mine), gram_pair, nothing, block_part)
    return (left_stat[None, None], right_stat[None, None])


def solution(mesh):
    in_specs = (
        P(("seq", "head"), None),
        P("seq", "head"),
        P("seq", "head"),
        P("seq", "head"),
        P("seq", "head"),
        P("seq"),
        P(),
    )
    out_specs = (P("seq", "head", None, None), P("seq", "head", None, None))
    return jax.shard_map(
        per_device, mesh=mesh, in_specs=in_specs, out_specs=out_specs, check_vma=False
    )
```

```python
import jax
import jax.numpy as jnp
from jax import lax
from jax.sharding import PartitionSpec as P
from jax.experimental import pallas as pl
from jax.experimental.pallas import tpu as pltpu

D = 5376
HD = 128
KV_DEV = 2
QPK = 2
WINDOW = 1024
BLOCK = 1024
NBLK = 6


score_scale = 168.0 ** (-0.5)
rotary_frequency_base = 10000.0
neg_large = -1e30
QBLK = 256


def attention_kernel(band_ref, q_ref, do_ref, k_ref, v_ref, dq_ref, dk_ref, dv_ref):
    tok_rows = q_ref.shape[0]
    span = QBLK + WINDOW
    dk_ref[...] = jnp.zeros(dk_ref.shape, jnp.float32)
    dv_ref[...] = jnp.zeros(dv_ref.shape, jnp.float32)
    def one_block(qb, carry):
        q0 = pl.multiple_of(qb * QBLK, QBLK)
        band = band_ref[pl.ds(q0, QBLK), :]
        band = jnp.concatenate([band, band], 0)
        col = lax.broadcasted_iota(jnp.int32, (QPK * QBLK, span), 1)
        row = lax.broadcasted_iota(jnp.int32, (QPK * QBLK, span), 0) % QBLK
        allowed = (col + q0 >= band) & (col <= row + WINDOW)
        for g in range(1):
            base = 0
            qs = jnp.concatenate(
                [q_ref[pl.ds(q0, QBLK), base + r * HD:base + (r + 1) * HD] for r in range(QPK)], 0)
            dos = jnp.concatenate(
                [do_ref[pl.ds(q0, QBLK), base + r * HD:base + (r + 1) * HD] for r in range(QPK)], 0)
            keys = k_ref[pl.ds(q0, span), g * HD:(g + 1) * HD]
            vals = v_ref[pl.ds(q0, span), g * HD:(g + 1) * HD]
            logits = lax.dot_general(qs, keys, (((1,), (1,)), ((), ())),
                                     preferred_element_type=jnp.float32) * score_scale
            masked = jnp.where(allowed, logits, neg_large)
            top = jnp.max(masked, -1, keepdims=True)
            expo = jnp.where(allowed, jnp.exp(masked - top), 0.0)
            attend = expo / jnp.sum(expo, -1, keepdims=True)
            grad_attend = lax.dot_general(dos, vals, (((1,), (1,)), ((), ())),
                                          preferred_element_type=jnp.float32)
            row_dot = jnp.sum(attend * grad_attend, -1, keepdims=True)
            grad_score = (attend * (grad_attend - row_dot) * score_scale).astype(jnp.bfloat16)
            dqs = jnp.dot(grad_score, keys, preferred_element_type=jnp.float32)
            for r in range(QPK):
                dq_ref[pl.ds(q0, QBLK), base + r * HD:base + (r + 1) * HD] = dqs[r * QBLK:(r + 1) * QBLK]
            dk_ref[pl.ds(q0, span), g * HD:(g + 1) * HD] += lax.dot_general(
                grad_score, qs, (((0,), (0,)), ((), ())), preferred_element_type=jnp.float32)
            dv_ref[pl.ds(q0, span), g * HD:(g + 1) * HD] += lax.dot_general(
                attend.astype(jnp.bfloat16), dos, (((0,), (0,)), ((), ())),
                preferred_element_type=jnp.float32)
        return carry

    lax.fori_loop(0, tok_rows // QBLK, one_block, 0)


def attention_backward(band_rel, queries, out_grad, key_all, value_all):
    tok_rows = queries.shape[0]
    head_cols = pl.BlockSpec((tok_rows, QPK * HD), lambda g: (0, g))
    kv_cols = pl.BlockSpec((2 * tok_rows, HD), lambda g: (0, g))
    band_spec = pl.BlockSpec((tok_rows, 1), lambda g: (0, 0))
    return pl.pallas_call(
        attention_kernel,
        grid=(KV_DEV,),
        out_shape=(
            jax.ShapeDtypeStruct(queries.shape, jnp.float32),
            jax.ShapeDtypeStruct(key_all.shape, jnp.float32),
            jax.ShapeDtypeStruct(value_all.shape, jnp.float32),
        ),
        in_specs=[band_spec, head_cols, head_cols, kv_cols, kv_cols],
        out_specs=(head_cols, kv_cols, kv_cols),
    )(band_rel.reshape(tok_rows, 1), queries, out_grad, key_all, value_all)


def shifted(value, axis, steps):
    count = lax.axis_size(axis)
    initial, last = (max(0, -steps), min(count, count - steps))
    return lax.ppermute(value, axis, [(source, source + steps) for source in range(initial, last)])


def rope_tables(positions, head_size):
    half_size = head_size // 2
    frequency = jnp.power(
        rotary_frequency_base, -2.0 * jnp.arange(half_size, dtype=jnp.float32) / head_size
    )
    angles = positions.astype(jnp.float32)[:, None] * frequency[None, :]
    cosine_table = jnp.concatenate([jnp.cos(angles), jnp.cos(angles)], 1)
    sine_table = jnp.concatenate([jnp.sin(angles), jnp.sin(angles)], 1)
    return (cosine_table, sine_table)


def unrotate(gradient, cosine_table, sine_table):
    half_size = gradient.shape[-1] // 2
    scaled = gradient * sine_table
    turned = jnp.concatenate([-scaled[..., half_size:], scaled[..., :half_size]], -1)
    return gradient * cosine_table - turned


def arrange_features(rows, seq_count):
    full_blocks = D // BLOCK
    piece = BLOCK // seq_count
    tail_piece = (D - full_blocks * BLOCK) // seq_count
    count = rows.shape[0]
    main = rows[:, : full_blocks * BLOCK].reshape(count, full_blocks, seq_count, piece)
    main = main.transpose(0, 2, 1, 3).reshape(count, seq_count, full_blocks * piece)
    tail = rows[:, full_blocks * BLOCK :].reshape(count, seq_count, tail_piece)
    return jnp.concatenate([main, tail], 2).reshape(count, D)


def owned_block(mine, owner_row, block_pick, seq_count):
    full_blocks = D // BLOCK
    piece = BLOCK // seq_count
    tail_piece = (D - full_blocks * BLOCK) // seq_count
    columns = mine.shape[1]
    mine = jnp.concatenate(
        [mine, jnp.zeros((NBLK * piece - mine.shape[0], columns), mine.dtype)], 0
    ).reshape(NBLK, piece, columns)
    destinations = jnp.arange(seq_count, dtype=jnp.int32)
    dest_block = jnp.sum(
        jnp.where(
            owner_row[None, :] == destinations[:, None],
            jnp.arange(NBLK, dtype=jnp.int32)[None, :],
            0,
        ),
        1,
    )
    send = jnp.take(mine, dest_block, axis=0)
    received = lax.all_to_all(send, "seq", 0, 0, tiled=False)
    main_block = received.reshape(BLOCK, columns)
    tail_block = jnp.concatenate(
        [
            received[:, :tail_piece].reshape(tail_piece * seq_count, columns),
            jnp.zeros((BLOCK - tail_piece * seq_count, columns), received.dtype),
        ],
        0,
    )
    return jnp.where(block_pick == full_blocks, tail_block, main_block)

def per_device(inputs, queries, key_rows, values, out_grad, band_start, owners):
    tok_rows = queries.shape[0]
    seq_count = lax.axis_size("seq")
    seq_index = lax.axis_index("seq")
    group_index = lax.axis_index("head")
    tokens_all = tok_rows * seq_count
    earlier_keys, earlier_values = shifted((key_rows, values), "seq", 1)
    key_all = jnp.concatenate([earlier_keys, key_rows], 0)
    value_all = jnp.concatenate([earlier_values, values], 0)
    band_rel = band_start - (seq_index * tok_rows - WINDOW)
    grad_query, grad_keys, grad_values = attention_backward(
        band_rel, queries, out_grad, key_all, value_all
    )
    grad_keys = grad_keys.reshape(2 * tok_rows, KV_DEV, HD)
    grad_values = grad_values.reshape(2 * tok_rows, KV_DEV, HD)
    rim_keys, rim_values = (
        shifted(grad_keys[:tok_rows].astype(jnp.bfloat16), "seq", -1).astype(jnp.float32),
        shifted(grad_values[:tok_rows].astype(jnp.bfloat16), "seq", -1).astype(jnp.float32),
    )
    own_keys = grad_keys[tok_rows:] + rim_keys
    own_values = grad_values[tok_rows:] + rim_values
    positions = seq_index * tok_rows + jnp.arange(tok_rows, dtype=jnp.int32)
    cosine_table, sine_table = rope_tables(positions, HD)
    query_pre = unrotate(
        grad_query.reshape(tok_rows, KV_DEV * QPK, HD),
        cosine_table[:, None, :],
        sine_table[:, None, :],
    )
    key_pre = unrotate(own_keys, cosine_table[:, None, :], sine_table[:, None, :])
    column_grads = jnp.concatenate(
        [
            query_pre.reshape(tok_rows, KV_DEV * QPK * HD),
            key_pre.reshape(tok_rows, KV_DEV * HD),
            own_values.reshape(tok_rows, KV_DEV * HD),
        ],
        1,
    ).astype(jnp.bfloat16)
    column_count = column_grads.shape[1]
    core = seq_index % 2
    paired = arrange_features(inputs, seq_count).reshape(inputs.shape[0], seq_count // 2, 2, -1)
    local = jnp.concatenate(
        [
            lax.dynamic_index_in_dim(paired, 1 - core, 2, keepdims=False),
            lax.dynamic_index_in_dim(paired, core, 2, keepdims=False),
        ],
        1,
    ).reshape(inputs.shape[0], D)
    head_count = lax.axis_size("head")
    lane_count = head_count // 2
    partner = lax.ppermute(
        local, "head", [(src, (src + lane_count) % head_count) for src in range(head_count)]
    )
    upper = group_index // lane_count
    pair = jnp.where(upper == 0, jnp.stack([local, partner]), jnp.stack([partner, local]))
    lanes = [list(range(start, start + lane_count)) for start in (0, lane_count)]
    gathered = lax.all_gather(pair, "head", axis=0, tiled=False, axis_index_groups=lanes)
    gathered = gathered.reshape(-1, D)
    column_grads = (
        column_grads.reshape(2, lane_count, inputs.shape[0], -1)
        .transpose(1, 0, 2, 3)
        .reshape(column_grads.shape)
    )
    half = D // 2
    given = lax.dot_general(
        gathered[:, :half], column_grads, (((0,), (0,)), ((), ())),
        preferred_element_type=jnp.float32,
    ).astype(jnp.bfloat16)
    taken = lax.ppermute(given, "seq", [(src, src ^ 1) for src in range(seq_count)])
    kept = lax.dot_general(
        gathered[:, half:], column_grads, (((0,), (0,)), ((), ())),
        preferred_element_type=jnp.float32,
    ).astype(jnp.bfloat16)
    kept, taken = lax.optimization_barrier((kept, taken))
    summed = (kept.astype(jnp.float32) + taken.astype(jnp.float32)).astype(jnp.bfloat16)
    groups = [list(range(parity, seq_count, 2)) for parity in range(2)]
    mine = lax.psum_scatter(
        summed, "seq", scatter_dimension=0, tiled=True, axis_index_groups=groups
    )
    owner_row = lax.dynamic_index_in_dim(owners, group_index, 0, keepdims=False)
    is_mine = owner_row == seq_index
    block_pick = jnp.sum(jnp.where(is_mine, jnp.arange(NBLK, dtype=jnp.int32), 0))
    block_part = owned_block(mine, owner_row, block_pick, seq_count)
    def gram_pair(part_rows):
        left_value = (
            lax.dot_general(
                part_rows, part_rows, (((1,), (1,)), ((), ())), preferred_element_type=jnp.float32
            )
            / tokens_all
        )
        right_value = (
            lax.dot_general(
                part_rows, part_rows, (((0,), (0,)), ((), ())), preferred_element_type=jnp.float32
            )
            / tokens_all
        )
        return (left_value, right_value)

    def nothing(part_rows):
        return (
            jnp.zeros((BLOCK, BLOCK), jnp.float32),
            jnp.zeros((column_count, column_count), jnp.float32),
        )

    left_stat, right_stat = lax.cond(jnp.any(is_mine), gram_pair, nothing, block_part)
    return (left_stat[None, None], right_stat[None, None])


def solution(mesh):
    in_specs = (
        P(("seq", "head"), None),
        P("seq", "head"),
        P("seq", "head"),
        P("seq", "head"),
        P("seq", "head"),
        P("seq"),
        P(),
    )
    out_specs = (P("seq", "head", None, None), P("seq", "head", None, None))
    return jax.shard_map(
        per_device, mesh=mesh, in_specs=in_specs, out_specs=out_specs, check_vma=False
    )
```

```python
import jax
import jax.numpy as jnp
from jax import lax
from jax.sharding import PartitionSpec as P
from jax.experimental import pallas as pl
from jax.experimental.pallas import tpu as pltpu

D = 5376
HD = 128
KV_DEV = 2
QPK = 2
WINDOW = 1024
BLOCK = 1024
NBLK = 6


score_scale = 168.0 ** (-0.5)
rotary_frequency_base = 10000.0
neg_large = -1e30
QBLK = 256


def attention_kernel(band_ref, q_ref, do_ref, k_ref, v_ref, dq_ref, dk_ref, dv_ref):
    tok_rows = q_ref.shape[0]
    span = QBLK + WINDOW
    dk_ref[...] = jnp.zeros(dk_ref.shape, jnp.float32)
    dv_ref[...] = jnp.zeros(dv_ref.shape, jnp.float32)
    def one_block(qb, carry):
        q0 = pl.multiple_of(qb * QBLK, QBLK)
        band = band_ref[pl.ds(q0, QBLK), :]
        band = jnp.concatenate([band, band], 0)
        col = lax.broadcasted_iota(jnp.int32, (QPK * QBLK, span), 1)
        row = lax.broadcasted_iota(jnp.int32, (QPK * QBLK, span), 0) % QBLK
        allowed = (col + q0 >= band) & (col <= row + WINDOW)
        for g in range(1):
            base = 0
            qs = jnp.concatenate(
                [q_ref[pl.ds(q0, QBLK), base + r * HD:base + (r + 1) * HD] for r in range(QPK)], 0)
            dos = jnp.concatenate(
                [do_ref[pl.ds(q0, QBLK), base + r * HD:base + (r + 1) * HD] for r in range(QPK)], 0)
            keys = k_ref[pl.ds(q0, span), g * HD:(g + 1) * HD]
            vals = v_ref[pl.ds(q0, span), g * HD:(g + 1) * HD]
            logits = lax.dot_general(qs, keys, (((1,), (1,)), ((), ())),
                                     preferred_element_type=jnp.float32) * score_scale
            masked = jnp.where(allowed, logits, neg_large)
            top = jnp.max(masked, -1, keepdims=True)
            expo = jnp.where(allowed, jnp.exp(masked - top), 0.0)
            attend = expo / jnp.sum(expo, -1, keepdims=True)
            grad_attend = lax.dot_general(dos, vals, (((1,), (1,)), ((), ())),
                                          preferred_element_type=jnp.float32)
            row_dot = jnp.sum(attend * grad_attend, -1, keepdims=True)
            grad_score = (attend * (grad_attend - row_dot) * score_scale).astype(jnp.bfloat16)
            dqs = jnp.dot(grad_score, keys, preferred_element_type=jnp.float32)
            for r in range(QPK):
                dq_ref[pl.ds(q0, QBLK), base + r * HD:base + (r + 1) * HD] = dqs[r * QBLK:(r + 1) * QBLK]
            dk_ref[pl.ds(q0, span), g * HD:(g + 1) * HD] += lax.dot_general(
                grad_score, qs, (((0,), (0,)), ((), ())), preferred_element_type=jnp.float32)
            dv_ref[pl.ds(q0, span), g * HD:(g + 1) * HD] += lax.dot_general(
                attend.astype(jnp.bfloat16), dos, (((0,), (0,)), ((), ())),
                preferred_element_type=jnp.float32)
        return carry

    lax.fori_loop(0, tok_rows // QBLK, one_block, 0)


def attention_backward(band_rel, queries, out_grad, key_all, value_all):
    tok_rows = queries.shape[0]
    head_cols = pl.BlockSpec((tok_rows, QPK * HD), lambda g: (0, g))
    kv_cols = pl.BlockSpec((2 * tok_rows, HD), lambda g: (0, g))
    band_spec = pl.BlockSpec((tok_rows, 1), lambda g: (0, 0))
    return pl.pallas_call(
        attention_kernel,
        grid=(KV_DEV,),
        out_shape=(
            jax.ShapeDtypeStruct(queries.shape, jnp.float32),
            jax.ShapeDtypeStruct(key_all.shape, jnp.float32),
            jax.ShapeDtypeStruct(value_all.shape, jnp.float32),
        ),
        in_specs=[band_spec, head_cols, head_cols, kv_cols, kv_cols],
        out_specs=(head_cols, kv_cols, kv_cols),
    )(band_rel.reshape(tok_rows, 1), queries, out_grad, key_all, value_all)


def shifted(value, axis, steps):
    count = lax.axis_size(axis)
    initial, last = (max(0, -steps), min(count, count - steps))
    return lax.ppermute(value, axis, [(source, source + steps) for source in range(initial, last)])


def rope_tables(positions, head_size):
    half_size = head_size // 2
    frequency = jnp.power(
        rotary_frequency_base, -2.0 * jnp.arange(half_size, dtype=jnp.float32) / head_size
    )
    angles = positions.astype(jnp.float32)[:, None] * frequency[None, :]
    cosine_table = jnp.concatenate([jnp.cos(angles), jnp.cos(angles)], 1)
    sine_table = jnp.concatenate([jnp.sin(angles), jnp.sin(angles)], 1)
    return (cosine_table, sine_table)


def unrotate(gradient, cosine_table, sine_table):
    half_size = gradient.shape[-1] // 2
    scaled = gradient * sine_table
    turned = jnp.concatenate([-scaled[..., half_size:], scaled[..., :half_size]], -1)
    return gradient * cosine_table - turned


def arrange_features(rows, seq_count):
    full_blocks = D // BLOCK
    piece = BLOCK // seq_count
    tail_piece = (D - full_blocks * BLOCK) // seq_count
    count = rows.shape[0]
    main = rows[:, : full_blocks * BLOCK].reshape(count, full_blocks, seq_count, piece)
    main = main.transpose(0, 2, 1, 3).reshape(count, seq_count, full_blocks * piece)
    tail = rows[:, full_blocks * BLOCK :].reshape(count, seq_count, tail_piece)
    return jnp.concatenate([main, tail], 2).reshape(count, D)


def owned_block(mine, owner_row, block_pick, seq_count):
    full_blocks = D // BLOCK
    piece = BLOCK // seq_count
    tail_piece = (D - full_blocks * BLOCK) // seq_count
    columns = mine.shape[1]
    mine = jnp.concatenate(
        [mine, jnp.zeros((NBLK * piece - mine.shape[0], columns), mine.dtype)], 0
    ).reshape(NBLK, piece, columns)
    destinations = jnp.arange(seq_count, dtype=jnp.int32)
    dest_block = jnp.sum(
        jnp.where(
            owner_row[None, :] == destinations[:, None],
            jnp.arange(NBLK, dtype=jnp.int32)[None, :],
            0,
        ),
        1,
    )
    send = jnp.take(mine, dest_block, axis=0)
    received = lax.all_to_all(send, "seq", 0, 0, tiled=False)
    main_block = received.reshape(BLOCK, columns)
    tail_block = jnp.concatenate(
        [
            received[:, :tail_piece].reshape(tail_piece * seq_count, columns),
            jnp.zeros((BLOCK - tail_piece * seq_count, columns), received.dtype),
        ],
        0,
    )
    return jnp.where(block_pick == full_blocks, tail_block, main_block)

def per_device(inputs, queries, key_rows, values, out_grad, band_start, owners):
    tok_rows = queries.shape[0]
    seq_count = lax.axis_size("seq")
    seq_index = lax.axis_index("seq")
    group_index = lax.axis_index("head")
    tokens_all = tok_rows * seq_count
    earlier_keys, earlier_values = shifted((key_rows, values), "seq", 1)
    key_all = jnp.concatenate([earlier_keys, key_rows], 0)
    value_all = jnp.concatenate([earlier_values, values], 0)
    band_rel = band_start - (seq_index * tok_rows - WINDOW)
    grad_query, grad_keys, grad_values = attention_backward(
        band_rel, queries, out_grad, key_all, value_all
    )
    grad_keys = grad_keys.reshape(2 * tok_rows, KV_DEV, HD)
    grad_values = grad_values.reshape(2 * tok_rows, KV_DEV, HD)
    rim_keys, rim_values = (
        shifted(grad_keys[:tok_rows].astype(jnp.bfloat16), "seq", -1).astype(jnp.float32),
        shifted(grad_values[:tok_rows].astype(jnp.bfloat16), "seq", -1).astype(jnp.float32),
    )
    own_keys = grad_keys[tok_rows:] + rim_keys
    own_values = grad_values[tok_rows:] + rim_values
    positions = seq_index * tok_rows + jnp.arange(tok_rows, dtype=jnp.int32)
    cosine_table, sine_table = rope_tables(positions, HD)
    query_pre = unrotate(
        grad_query.reshape(tok_rows, KV_DEV * QPK, HD),
        cosine_table[:, None, :],
        sine_table[:, None, :],
    )
    key_pre = unrotate(own_keys, cosine_table[:, None, :], sine_table[:, None, :])
    column_grads = jnp.concatenate(
        [
            query_pre.reshape(tok_rows, KV_DEV * QPK * HD),
            key_pre.reshape(tok_rows, KV_DEV * HD),
            own_values.reshape(tok_rows, KV_DEV * HD),
        ],
        1,
    ).astype(jnp.bfloat16)
    column_count = column_grads.shape[1]
    core = seq_index % 2
    paired = arrange_features(inputs, seq_count).reshape(inputs.shape[0], seq_count // 2, 2, -1)
    local = jnp.concatenate(
        [
            lax.dynamic_index_in_dim(paired, 1 - core, 2, keepdims=False),
            lax.dynamic_index_in_dim(paired, core, 2, keepdims=False),
        ],
        1,
    ).reshape(inputs.shape[0], D)
    head_count = lax.axis_size("head")
    lane_count = head_count // 2
    split = D // 2
    direct = lax.ppermute(
        local[:, :split], "head",
        [(src, (src + lane_count) % head_count) for src in range(head_count)],
    )
    relay_pairs = []
    for seq_at in range(seq_count):
        for head_at in range(head_count):
            z_here = (head_at // lane_count) * 2 + seq_at // (seq_count // 2)
            z_next = (z_here - 1) % 4
            seq_next = (z_next % 2) * (seq_count // 2) + seq_at % (seq_count // 2)
            head_next = (z_next // 2) * lane_count + head_at % lane_count
            relay_pairs.append((seq_at * head_count + head_at, seq_next * head_count + head_next))
    relayed = local[:, split:]
    for hop in range(2):
        relayed = lax.ppermute(relayed, ("seq", "head"), relay_pairs)
    partner = jnp.concatenate([direct, relayed], 1)
    upper = group_index // lane_count
    pair = jnp.where(upper == 0, jnp.stack([local, partner]), jnp.stack([partner, local]))
    lanes = [list(range(start, start + lane_count)) for start in (0, lane_count)]
    gathered = lax.all_gather(pair, "head", axis=0, tiled=False, axis_index_groups=lanes)
    gathered = gathered.reshape(-1, D)
    column_grads = (
        column_grads.reshape(2, lane_count, inputs.shape[0], -1)
        .transpose(1, 0, 2, 3)
        .reshape(column_grads.shape)
    )
    half = D // 2
    given = lax.dot_general(
        gathered[:, :half], column_grads, (((0,), (0,)), ((), ())),
        preferred_element_type=jnp.float32,
    ).astype(jnp.bfloat16)
    taken = lax.ppermute(given, "seq", [(src, src ^ 1) for src in range(seq_count)])
    kept = lax.dot_general(
        gathered[:, half:], column_grads, (((0,), (0,)), ((), ())),
        preferred_element_type=jnp.float32,
    ).astype(jnp.bfloat16)
    kept, taken = lax.optimization_barrier((kept, taken))
    summed = (kept.astype(jnp.float32) + taken.astype(jnp.float32)).astype(jnp.bfloat16)
    groups = [list(range(parity, seq_count, 2)) for parity in range(2)]
    mine = lax.psum_scatter(
        summed, "seq", scatter_dimension=0, tiled=True, axis_index_groups=groups
    )
    owner_row = lax.dynamic_index_in_dim(owners, group_index, 0, keepdims=False)
    is_mine = owner_row == seq_index
    block_pick = jnp.sum(jnp.where(is_mine, jnp.arange(NBLK, dtype=jnp.int32), 0))
    block_part = owned_block(mine, owner_row, block_pick, seq_count)
    def gram_pair(part_rows):
        left_value = (
            lax.dot_general(
                part_rows, part_rows, (((1,), (1,)), ((), ())), preferred_element_type=jnp.float32
            )
            / tokens_all
        )
        right_value = (
            lax.dot_general(
                part_rows, part_rows, (((0,), (0,)), ((), ())), preferred_element_type=jnp.float32
            )
            / tokens_all
        )
        return (left_value, right_value)

    def nothing(part_rows):
        return (
            jnp.zeros((BLOCK, BLOCK), jnp.float32),
            jnp.zeros((column_count, column_count), jnp.float32),
        )

    left_stat, right_stat = lax.cond(jnp.any(is_mine), gram_pair, nothing, block_part)
    return (left_stat[None, None], right_stat[None, None])


def solution(mesh):
    in_specs = (
        P(("seq", "head"), None),
        P("seq", "head"),
        P("seq", "head"),
        P("seq", "head"),
        P("seq", "head"),
        P("seq"),
        P(),
    )
    out_specs = (P("seq", "head", None, None), P("seq", "head", None, None))
    return jax.shard_map(
        per_device, mesh=mesh, in_specs=in_specs, out_specs=out_specs, check_vma=False
    )
```

```python
import jax
import jax.numpy as jnp
from jax import lax
from jax.sharding import PartitionSpec as P
from jax.experimental import pallas as pl
from jax.experimental.pallas import tpu as pltpu

D = 5376
HD = 128
KV_DEV = 2
QPK = 2
WINDOW = 1024
BLOCK = 1024
NBLK = 6


score_scale = 168.0 ** (-0.5)
rotary_frequency_base = 10000.0
neg_large = -1e30
QBLK = 256


def attention_kernel(band_ref, q_ref, do_ref, k_ref, v_ref, dq_ref, dk_ref, dv_ref):
    tok_rows = q_ref.shape[0]
    span = QBLK + WINDOW
    dk_ref[...] = jnp.zeros(dk_ref.shape, jnp.float32)
    dv_ref[...] = jnp.zeros(dv_ref.shape, jnp.float32)
    def one_block(qb, carry):
        q0 = pl.multiple_of(qb * QBLK, QBLK)
        band = band_ref[pl.ds(q0, QBLK), :]
        band = jnp.concatenate([band, band], 0)
        col = lax.broadcasted_iota(jnp.int32, (QPK * QBLK, span), 1)
        row = lax.broadcasted_iota(jnp.int32, (QPK * QBLK, span), 0) % QBLK
        allowed = (col + q0 >= band) & (col <= row + WINDOW)
        for g in range(1):
            base = 0
            qs = jnp.concatenate(
                [q_ref[pl.ds(q0, QBLK), base + r * HD:base + (r + 1) * HD] for r in range(QPK)], 0)
            dos = jnp.concatenate(
                [do_ref[pl.ds(q0, QBLK), base + r * HD:base + (r + 1) * HD] for r in range(QPK)], 0)
            keys = k_ref[pl.ds(q0, span), g * HD:(g + 1) * HD]
            vals = v_ref[pl.ds(q0, span), g * HD:(g + 1) * HD]
            logits = lax.dot_general(qs, keys, (((1,), (1,)), ((), ())),
                                     preferred_element_type=jnp.float32) * score_scale
            masked = jnp.where(allowed, logits, neg_large)
            top = jnp.max(masked, -1, keepdims=True)
            expo = jnp.where(allowed, jnp.exp(masked - top), 0.0)
            attend = expo / jnp.sum(expo, -1, keepdims=True)
            grad_attend = lax.dot_general(dos, vals, (((1,), (1,)), ((), ())),
                                          preferred_element_type=jnp.float32)
            row_dot = jnp.sum(attend * grad_attend, -1, keepdims=True)
            grad_score = (attend * (grad_attend - row_dot) * score_scale).astype(jnp.bfloat16)
            dqs = jnp.dot(grad_score, keys, preferred_element_type=jnp.float32)
            for r in range(QPK):
                dq_ref[pl.ds(q0, QBLK), base + r * HD:base + (r + 1) * HD] = dqs[r * QBLK:(r + 1) * QBLK]
            dk_ref[pl.ds(q0, span), g * HD:(g + 1) * HD] += lax.dot_general(
                grad_score, qs, (((0,), (0,)), ((), ())), preferred_element_type=jnp.float32)
            dv_ref[pl.ds(q0, span), g * HD:(g + 1) * HD] += lax.dot_general(
                attend.astype(jnp.bfloat16), dos, (((0,), (0,)), ((), ())),
                preferred_element_type=jnp.float32)
        return carry

    lax.fori_loop(0, tok_rows // QBLK, one_block, 0)


def attention_backward(band_rel, queries, out_grad, key_all, value_all):
    tok_rows = queries.shape[0]
    head_cols = pl.BlockSpec((tok_rows, QPK * HD), lambda g: (0, g))
    kv_cols = pl.BlockSpec((2 * tok_rows, HD), lambda g: (0, g))
    band_spec = pl.BlockSpec((tok_rows, 1), lambda g: (0, 0))
    return pl.pallas_call(
        attention_kernel,
        grid=(KV_DEV,),
        out_shape=(
            jax.ShapeDtypeStruct(queries.shape, jnp.float32),
            jax.ShapeDtypeStruct(key_all.shape, jnp.float32),
            jax.ShapeDtypeStruct(value_all.shape, jnp.float32),
        ),
        in_specs=[band_spec, head_cols, head_cols, kv_cols, kv_cols],
        out_specs=(head_cols, kv_cols, kv_cols),
    )(band_rel.reshape(tok_rows, 1), queries, out_grad, key_all, value_all)


def shifted(value, axis, steps):
    count = lax.axis_size(axis)
    initial, last = (max(0, -steps), min(count, count - steps))
    return lax.ppermute(value, axis, [(source, source + steps) for source in range(initial, last)])


def rope_tables(positions, head_size):
    half_size = head_size // 2
    frequency = jnp.power(
        rotary_frequency_base, -2.0 * jnp.arange(half_size, dtype=jnp.float32) / head_size
    )
    angles = positions.astype(jnp.float32)[:, None] * frequency[None, :]
    cosine_table = jnp.concatenate([jnp.cos(angles), jnp.cos(angles)], 1)
    sine_table = jnp.concatenate([jnp.sin(angles), jnp.sin(angles)], 1)
    return (cosine_table, sine_table)


def unrotate(gradient, cosine_table, sine_table):
    half_size = gradient.shape[-1] // 2
    scaled = gradient * sine_table
    turned = jnp.concatenate([-scaled[..., half_size:], scaled[..., :half_size]], -1)
    return gradient * cosine_table - turned


def arrange_features(rows, seq_count):
    full_blocks = D // BLOCK
    piece = BLOCK // seq_count
    tail_piece = (D - full_blocks * BLOCK) // seq_count
    count = rows.shape[0]
    main = rows[:, : full_blocks * BLOCK].reshape(count, full_blocks, seq_count, piece)
    main = main.transpose(0, 2, 1, 3).reshape(count, seq_count, full_blocks * piece)
    tail = rows[:, full_blocks * BLOCK :].reshape(count, seq_count, tail_piece)
    return jnp.concatenate([main, tail], 2).reshape(count, D)


def owned_block(mine, owner_row, block_pick, seq_count):
    full_blocks = D // BLOCK
    piece = BLOCK // seq_count
    tail_piece = (D - full_blocks * BLOCK) // seq_count
    columns = mine.shape[1]
    mine = jnp.concatenate(
        [mine, jnp.zeros((NBLK * piece - mine.shape[0], columns), mine.dtype)], 0
    ).reshape(NBLK, piece, columns)
    destinations = jnp.arange(seq_count, dtype=jnp.int32)
    dest_block = jnp.sum(
        jnp.where(
            owner_row[None, :] == destinations[:, None],
            jnp.arange(NBLK, dtype=jnp.int32)[None, :],
            0,
        ),
        1,
    )
    send = jnp.take(mine, dest_block, axis=0)
    received = lax.all_to_all(send, "seq", 0, 0, tiled=False)
    main_block = received.reshape(BLOCK, columns)
    tail_block = jnp.concatenate(
        [
            received[:, :tail_piece].reshape(tail_piece * seq_count, columns),
            jnp.zeros((BLOCK - tail_piece * seq_count, columns), received.dtype),
        ],
        0,
    )
    return jnp.where(block_pick == full_blocks, tail_block, main_block)

def per_device(inputs, queries, key_rows, values, out_grad, band_start, owners):
    tok_rows = queries.shape[0]
    seq_count = lax.axis_size("seq")
    seq_index = lax.axis_index("seq")
    group_index = lax.axis_index("head")
    tokens_all = tok_rows * seq_count
    earlier_keys, earlier_values = shifted((key_rows, values), "seq", 1)
    key_all = jnp.concatenate([earlier_keys, key_rows], 0)
    value_all = jnp.concatenate([earlier_values, values], 0)
    band_rel = band_start - (seq_index * tok_rows - WINDOW)
    grad_query, grad_keys, grad_values = attention_backward(
        band_rel, queries, out_grad, key_all, value_all
    )
    grad_keys = grad_keys.reshape(2 * tok_rows, KV_DEV, HD)
    grad_values = grad_values.reshape(2 * tok_rows, KV_DEV, HD)
    rim_keys, rim_values = (
        shifted(grad_keys[:tok_rows].astype(jnp.bfloat16), "seq", -1).astype(jnp.float32),
        shifted(grad_values[:tok_rows].astype(jnp.bfloat16), "seq", -1).astype(jnp.float32),
    )
    own_keys = grad_keys[tok_rows:] + rim_keys
    own_values = grad_values[tok_rows:] + rim_values
    positions = seq_index * tok_rows + jnp.arange(tok_rows, dtype=jnp.int32)
    cosine_table, sine_table = rope_tables(positions, HD)
    query_pre = unrotate(
        grad_query.reshape(tok_rows, KV_DEV * QPK, HD),
        cosine_table[:, None, :],
        sine_table[:, None, :],
    )
    key_pre = unrotate(own_keys, cosine_table[:, None, :], sine_table[:, None, :])
    column_grads = jnp.concatenate(
        [
            query_pre.reshape(tok_rows, KV_DEV * QPK * HD),
            key_pre.reshape(tok_rows, KV_DEV * HD),
            own_values.reshape(tok_rows, KV_DEV * HD),
        ],
        1,
    ).astype(jnp.bfloat16)
    column_count = column_grads.shape[1]
    core = seq_index % 2
    paired = arrange_features(inputs, seq_count).reshape(inputs.shape[0], seq_count // 2, 2, -1)
    local = jnp.concatenate(
        [
            lax.dynamic_index_in_dim(paired, 1 - core, 2, keepdims=False),
            lax.dynamic_index_in_dim(paired, core, 2, keepdims=False),
        ],
        1,
    ).reshape(inputs.shape[0], D)
    head_count = lax.axis_size("head")
    lane_count = head_count // 2
    partner = lax.ppermute(
        local, "head", [(src, (src + lane_count) % head_count) for src in range(head_count)]
    )
    upper = group_index // lane_count
    pair = jnp.stack([local, partner])
    lanes = [list(range(start, start + lane_count)) for start in (0, lane_count)]
    gathered = lax.all_gather(pair, "head", axis=0, tiled=False, axis_index_groups=lanes)
    gathered = gathered.reshape(-1, D)
    halves = column_grads.reshape(2, lane_count, inputs.shape[0], -1)
    halves = lax.dynamic_slice_in_dim(jnp.concatenate([halves, halves], 0), upper, 2, 0)
    column_grads = halves.transpose(1, 0, 2, 3).reshape(column_grads.shape)
    half = D // 2
    given = lax.dot_general(
        gathered[:, :half], column_grads, (((0,), (0,)), ((), ())),
        preferred_element_type=jnp.float32,
    ).astype(jnp.bfloat16)
    taken = lax.ppermute(given, "seq", [(src, src ^ 1) for src in range(seq_count)])
    kept = lax.dot_general(
        gathered[:, half:], column_grads, (((0,), (0,)), ((), ())),
        preferred_element_type=jnp.float32,
    ).astype(jnp.bfloat16)
    kept, taken = lax.optimization_barrier((kept, taken))
    summed = (kept.astype(jnp.float32) + taken.astype(jnp.float32)).astype(jnp.bfloat16)
    groups = [list(range(parity, seq_count, 2)) for parity in range(2)]
    mine = lax.psum_scatter(
        summed, "seq", scatter_dimension=0, tiled=True, axis_index_groups=groups
    )
    owner_row = lax.dynamic_index_in_dim(owners, group_index, 0, keepdims=False)
    is_mine = owner_row == seq_index
    block_pick = jnp.sum(jnp.where(is_mine, jnp.arange(NBLK, dtype=jnp.int32), 0))
    block_part = owned_block(mine, owner_row, block_pick, seq_count)
    def gram_pair(part_rows):
        left_value = (
            lax.dot_general(
                part_rows, part_rows, (((1,), (1,)), ((), ())), preferred_element_type=jnp.float32
            )
            / tokens_all
        )
        right_value = (
            lax.dot_general(
                part_rows, part_rows, (((0,), (0,)), ((), ())), preferred_element_type=jnp.float32
            )
            / tokens_all
        )
        return (left_value, right_value)

    def nothing(part_rows):
        return (
            jnp.zeros((BLOCK, BLOCK), jnp.float32),
            jnp.zeros((column_count, column_count), jnp.float32),
        )

    left_stat, right_stat = lax.cond(jnp.any(is_mine), gram_pair, nothing, block_part)
    return (left_stat[None, None], right_stat[None, None])


def solution(mesh):
    in_specs = (
        P(("seq", "head"), None),
        P("seq", "head"),
        P("seq", "head"),
        P("seq", "head"),
        P("seq", "head"),
        P("seq"),
        P(),
    )
    out_specs = (P("seq", "head", None, None), P("seq", "head", None, None))
    return jax.shard_map(
        per_device, mesh=mesh, in_specs=in_specs, out_specs=out_specs, check_vma=False
    )
```

```python
import jax
import jax.numpy as jnp
from jax import lax
from jax.sharding import PartitionSpec as P
from jax.experimental import pallas as pl
from jax.experimental.pallas import tpu as pltpu

D = 5376
HD = 128
KV_DEV = 2
QPK = 2
WINDOW = 1024
BLOCK = 1024
NBLK = 6


score_scale = 168.0 ** (-0.5)
rotary_frequency_base = 10000.0
neg_large = -1e30
QBLK = 256


def attention_kernel(band_ref, q_ref, do_ref, k_ref, v_ref, dq_ref, dk_ref, dv_ref):
    tok_rows = q_ref.shape[0]
    span = QBLK + WINDOW
    dk_ref[...] = jnp.zeros(dk_ref.shape, jnp.float32)
    dv_ref[...] = jnp.zeros(dv_ref.shape, jnp.float32)
    def one_block(qb, carry):
        q0 = pl.multiple_of(qb * QBLK, QBLK)
        band = band_ref[pl.ds(q0, QBLK), :]
        band = jnp.concatenate([band, band], 0)
        col = lax.broadcasted_iota(jnp.int32, (QPK * QBLK, span), 1)
        row = lax.broadcasted_iota(jnp.int32, (QPK * QBLK, span), 0) % QBLK
        allowed = (col + q0 >= band) & (col <= row + WINDOW)
        for g in range(1):
            base = 0
            qs = jnp.concatenate(
                [q_ref[pl.ds(q0, QBLK), base + r * HD:base + (r + 1) * HD] for r in range(QPK)], 0)
            dos = jnp.concatenate(
                [do_ref[pl.ds(q0, QBLK), base + r * HD:base + (r + 1) * HD] for r in range(QPK)], 0)
            keys = k_ref[pl.ds(q0, span), g * HD:(g + 1) * HD]
            vals = v_ref[pl.ds(q0, span), g * HD:(g + 1) * HD]
            logits = lax.dot_general(qs, keys, (((1,), (1,)), ((), ())),
                                     preferred_element_type=jnp.float32) * score_scale
            masked = jnp.where(allowed, logits, neg_large)
            top = jnp.max(masked, -1, keepdims=True)
            expo = jnp.where(allowed, jnp.exp(masked - top), 0.0)
            attend = expo / jnp.sum(expo, -1, keepdims=True)
            grad_attend = lax.dot_general(dos, vals, (((1,), (1,)), ((), ())),
                                          preferred_element_type=jnp.float32)
            row_dot = jnp.sum(attend * grad_attend, -1, keepdims=True)
            grad_score = (attend * (grad_attend - row_dot) * score_scale).astype(jnp.bfloat16)
            dqs = jnp.dot(grad_score, keys, preferred_element_type=jnp.float32)
            for r in range(QPK):
                dq_ref[pl.ds(q0, QBLK), base + r * HD:base + (r + 1) * HD] = dqs[r * QBLK:(r + 1) * QBLK]
            dk_ref[pl.ds(q0, span), g * HD:(g + 1) * HD] += lax.dot_general(
                grad_score, qs, (((0,), (0,)), ((), ())), preferred_element_type=jnp.float32)
            dv_ref[pl.ds(q0, span), g * HD:(g + 1) * HD] += lax.dot_general(
                attend.astype(jnp.bfloat16), dos, (((0,), (0,)), ((), ())),
                preferred_element_type=jnp.float32)
        return carry

    lax.fori_loop(0, tok_rows // QBLK, one_block, 0)


def attention_backward(band_rel, queries, out_grad, key_all, value_all):
    tok_rows = queries.shape[0]
    head_cols = pl.BlockSpec((tok_rows, QPK * HD), lambda g: (0, g))
    kv_cols = pl.BlockSpec((2 * tok_rows, HD), lambda g: (0, g))
    band_spec = pl.BlockSpec((tok_rows, 1), lambda g: (0, 0))
    return pl.pallas_call(
        attention_kernel,
        grid=(KV_DEV,),
        out_shape=(
            jax.ShapeDtypeStruct(queries.shape, jnp.float32),
            jax.ShapeDtypeStruct(key_all.shape, jnp.float32),
            jax.ShapeDtypeStruct(value_all.shape, jnp.float32),
        ),
        in_specs=[band_spec, head_cols, head_cols, kv_cols, kv_cols],
        out_specs=(head_cols, kv_cols, kv_cols),
    )(band_rel.reshape(tok_rows, 1), queries, out_grad, key_all, value_all)


def shifted(value, axis, steps):
    count = lax.axis_size(axis)
    initial, last = (max(0, -steps), min(count, count - steps))
    return lax.ppermute(value, axis, [(source, source + steps) for source in range(initial, last)])


def rope_tables(positions, head_size):
    half_size = head_size // 2
    frequency = jnp.power(
        rotary_frequency_base, -2.0 * jnp.arange(half_size, dtype=jnp.float32) / head_size
    )
    angles = positions.astype(jnp.float32)[:, None] * frequency[None, :]
    cosine_table = jnp.concatenate([jnp.cos(angles), jnp.cos(angles)], 1)
    sine_table = jnp.concatenate([jnp.sin(angles), jnp.sin(angles)], 1)
    return (cosine_table, sine_table)


def unrotate(gradient, cosine_table, sine_table):
    half_size = gradient.shape[-1] // 2
    scaled = gradient * sine_table
    turned = jnp.concatenate([-scaled[..., half_size:], scaled[..., :half_size]], -1)
    return gradient * cosine_table - turned


def arrange_features(rows, seq_count):
    full_blocks = D // BLOCK
    piece = BLOCK // seq_count
    tail_piece = (D - full_blocks * BLOCK) // seq_count
    count = rows.shape[0]
    main = rows[:, : full_blocks * BLOCK].reshape(count, full_blocks, seq_count, piece)
    main = main.transpose(0, 2, 1, 3).reshape(count, seq_count, full_blocks * piece)
    tail = rows[:, full_blocks * BLOCK :].reshape(count, seq_count, tail_piece)
    return jnp.concatenate([main, tail], 2).reshape(count, D)


def owned_block(mine, owner_row, block_pick, seq_count):
    full_blocks = D // BLOCK
    piece = BLOCK // seq_count
    tail_piece = (D - full_blocks * BLOCK) // seq_count
    columns = mine.shape[1]
    mine = jnp.concatenate(
        [mine, jnp.zeros((NBLK * piece - mine.shape[0], columns), mine.dtype)], 0
    ).reshape(NBLK, piece, columns)
    destinations = jnp.arange(seq_count, dtype=jnp.int32)
    dest_block = jnp.sum(
        jnp.where(
            owner_row[None, :] == destinations[:, None],
            jnp.arange(NBLK, dtype=jnp.int32)[None, :],
            0,
        ),
        1,
    )
    send = jnp.take(mine, dest_block, axis=0)
    received = lax.all_to_all(send, "seq", 0, 0, tiled=False)
    main_block = received.reshape(BLOCK, columns)
    tail_block = jnp.concatenate(
        [
            received[:, :tail_piece].reshape(tail_piece * seq_count, columns),
            jnp.zeros((BLOCK - tail_piece * seq_count, columns), received.dtype),
        ],
        0,
    )
    return jnp.where(block_pick == full_blocks, tail_block, main_block)

def per_device(inputs, queries, key_rows, values, out_grad, band_start, owners):
    tok_rows = queries.shape[0]
    seq_count = lax.axis_size("seq")
    seq_index = lax.axis_index("seq")
    group_index = lax.axis_index("head")
    tokens_all = tok_rows * seq_count
    earlier_keys, earlier_values = shifted((key_rows, values), "seq", 1)
    key_all = jnp.concatenate([earlier_keys, key_rows], 0)
    value_all = jnp.concatenate([earlier_values, values], 0)
    band_rel = band_start - (seq_index * tok_rows - WINDOW)
    grad_query, grad_keys, grad_values = attention_backward(
        band_rel, queries, out_grad, key_all, value_all
    )
    grad_keys = grad_keys.reshape(2 * tok_rows, KV_DEV, HD)
    grad_values = grad_values.reshape(2 * tok_rows, KV_DEV, HD)
    rim_keys, rim_values = (
        shifted(grad_keys[:tok_rows].astype(jnp.bfloat16), "seq", -1).astype(jnp.float32),
        shifted(grad_values[:tok_rows].astype(jnp.bfloat16), "seq", -1).astype(jnp.float32),
    )
    own_keys = grad_keys[tok_rows:] + rim_keys
    own_values = grad_values[tok_rows:] + rim_values
    positions = seq_index * tok_rows + jnp.arange(tok_rows, dtype=jnp.int32)
    cosine_table, sine_table = rope_tables(positions, HD)
    query_pre = unrotate(
        grad_query.reshape(tok_rows, KV_DEV * QPK, HD),
        cosine_table[:, None, :],
        sine_table[:, None, :],
    )
    key_pre = unrotate(own_keys, cosine_table[:, None, :], sine_table[:, None, :])
    column_grads = jnp.concatenate(
        [
            query_pre.reshape(tok_rows, KV_DEV * QPK * HD),
            key_pre.reshape(tok_rows, KV_DEV * HD),
            own_values.reshape(tok_rows, KV_DEV * HD),
        ],
        1,
    ).astype(jnp.bfloat16)
    column_count = column_grads.shape[1]
    core = seq_index % 2
    head_count = lax.axis_size("head")
    lane_count = head_count // 2
    raw_partner = lax.ppermute(
        inputs, "head", [(src, (src + lane_count) % head_count) for src in range(head_count)]
    )

    def parity_order(rows):
        paired = arrange_features(rows, seq_count).reshape(rows.shape[0], seq_count // 2, 2, -1)
        return jnp.concatenate(
            [
                lax.dynamic_index_in_dim(paired, 1 - core, 2, keepdims=False),
                lax.dynamic_index_in_dim(paired, core, 2, keepdims=False),
            ],
            1,
        ).reshape(rows.shape[0], D)

    local = parity_order(inputs)
    partner = parity_order(raw_partner)
    upper = group_index // lane_count
    pair = jnp.stack([local, partner])
    lanes = [list(range(start, start + lane_count)) for start in (0, lane_count)]
    gathered = lax.all_gather(pair, "head", axis=0, tiled=False, axis_index_groups=lanes)
    gathered = gathered.reshape(-1, D)
    halves = column_grads.reshape(2, lane_count, inputs.shape[0], -1)
    halves = lax.dynamic_slice_in_dim(jnp.concatenate([halves, halves], 0), upper, 2, 0)
    column_grads = halves.transpose(1, 0, 2, 3).reshape(column_grads.shape)
    half = D // 2
    given = lax.dot_general(
        gathered[:, :half], column_grads, (((0,), (0,)), ((), ())),
        preferred_element_type=jnp.float32,
    ).astype(jnp.bfloat16)
    taken = lax.ppermute(given, "seq", [(src, src ^ 1) for src in range(seq_count)])
    kept = lax.dot_general(
        gathered[:, half:], column_grads, (((0,), (0,)), ((), ())),
        preferred_element_type=jnp.float32,
    ).astype(jnp.bfloat16)
    kept, taken = lax.optimization_barrier((kept, taken))
    summed = (kept.astype(jnp.float32) + taken.astype(jnp.float32)).astype(jnp.bfloat16)
    groups = [list(range(parity, seq_count, 2)) for parity in range(2)]
    mine = lax.psum_scatter(
        summed, "seq", scatter_dimension=0, tiled=True, axis_index_groups=groups
    )
    owner_row = lax.dynamic_index_in_dim(owners, group_index, 0, keepdims=False)
    is_mine = owner_row == seq_index
    block_pick = jnp.sum(jnp.where(is_mine, jnp.arange(NBLK, dtype=jnp.int32), 0))
    block_part = owned_block(mine, owner_row, block_pick, seq_count)
    def gram_pair(part_rows):
        left_value = (
            lax.dot_general(
                part_rows, part_rows, (((1,), (1,)), ((), ())), preferred_element_type=jnp.float32
            )
            / tokens_all
        )
        right_value = (
            lax.dot_general(
                part_rows, part_rows, (((0,), (0,)), ((), ())), preferred_element_type=jnp.float32
            )
            / tokens_all
        )
        return (left_value, right_value)

    def nothing(part_rows):
        return (
            jnp.zeros((BLOCK, BLOCK), jnp.float32),
            jnp.zeros((column_count, column_count), jnp.float32),
        )

    left_stat, right_stat = lax.cond(jnp.any(is_mine), gram_pair, nothing, block_part)
    return (left_stat[None, None], right_stat[None, None])


def solution(mesh):
    in_specs = (
        P(("seq", "head"), None),
        P("seq", "head"),
        P("seq", "head"),
        P("seq", "head"),
        P("seq", "head"),
        P("seq"),
        P(),
    )
    out_specs = (P("seq", "head", None, None), P("seq", "head", None, None))
    return jax.shard_map(
        per_device, mesh=mesh, in_specs=in_specs, out_specs=out_specs, check_vma=False
    )
```

```python
import jax
import jax.numpy as jnp
from jax import lax
from jax.sharding import PartitionSpec as P
from jax.experimental import pallas as pl
from jax.experimental.pallas import tpu as pltpu

D = 5376
HD = 128
KV_DEV = 2
QPK = 2
WINDOW = 1024
BLOCK = 1024
NBLK = 6


score_scale = 168.0 ** (-0.5)
rotary_frequency_base = 10000.0
neg_large = -1e30
QBLK = 256


def attention_kernel(band_ref, q_ref, do_ref, k_ref, v_ref, dq_ref, dk_ref, dv_ref):
    tok_rows = q_ref.shape[0]
    span = QBLK + WINDOW
    dk_ref[...] = jnp.zeros(dk_ref.shape, jnp.float32)
    dv_ref[...] = jnp.zeros(dv_ref.shape, jnp.float32)
    def one_block(qb, carry):
        q0 = pl.multiple_of(qb * QBLK, QBLK)
        band = band_ref[pl.ds(q0, QBLK), :]
        band = jnp.concatenate([band, band], 0)
        col = lax.broadcasted_iota(jnp.int32, (QPK * QBLK, span), 1)
        row = lax.broadcasted_iota(jnp.int32, (QPK * QBLK, span), 0) % QBLK
        allowed = (col + q0 >= band) & (col <= row + WINDOW)
        for g in range(1):
            base = 0
            qs = jnp.concatenate(
                [q_ref[pl.ds(q0, QBLK), base + r * HD:base + (r + 1) * HD] for r in range(QPK)], 0)
            dos = jnp.concatenate(
                [do_ref[pl.ds(q0, QBLK), base + r * HD:base + (r + 1) * HD] for r in range(QPK)], 0)
            keys = k_ref[pl.ds(q0, span), g * HD:(g + 1) * HD]
            vals = v_ref[pl.ds(q0, span), g * HD:(g + 1) * HD]
            logits = lax.dot_general(qs, keys, (((1,), (1,)), ((), ())),
                                     preferred_element_type=jnp.float32) * score_scale
            masked = jnp.where(allowed, logits, neg_large)
            top = jnp.max(masked, -1, keepdims=True)
            expo = jnp.where(allowed, jnp.exp(masked - top), 0.0)
            attend = expo / jnp.sum(expo, -1, keepdims=True)
            grad_attend = lax.dot_general(dos, vals, (((1,), (1,)), ((), ())),
                                          preferred_element_type=jnp.float32)
            row_dot = jnp.sum(attend * grad_attend, -1, keepdims=True)
            grad_score = (attend * (grad_attend - row_dot) * score_scale).astype(jnp.bfloat16)
            dqs = jnp.dot(grad_score, keys, preferred_element_type=jnp.float32)
            for r in range(QPK):
                dq_ref[pl.ds(q0, QBLK), base + r * HD:base + (r + 1) * HD] = dqs[r * QBLK:(r + 1) * QBLK]
            dk_ref[pl.ds(q0, span), g * HD:(g + 1) * HD] += lax.dot_general(
                grad_score, qs, (((0,), (0,)), ((), ())), preferred_element_type=jnp.float32)
            dv_ref[pl.ds(q0, span), g * HD:(g + 1) * HD] += lax.dot_general(
                attend.astype(jnp.bfloat16), dos, (((0,), (0,)), ((), ())),
                preferred_element_type=jnp.float32)
        return carry

    lax.fori_loop(0, tok_rows // QBLK, one_block, 0)


def attention_backward(band_rel, queries, out_grad, key_all, value_all):
    tok_rows = queries.shape[0]
    head_cols = pl.BlockSpec((tok_rows, QPK * HD), lambda g: (0, g))
    kv_cols = pl.BlockSpec((2 * tok_rows, HD), lambda g: (0, g))
    band_spec = pl.BlockSpec((tok_rows, 1), lambda g: (0, 0))
    return pl.pallas_call(
        attention_kernel,
        grid=(KV_DEV,),
        out_shape=(
            jax.ShapeDtypeStruct(queries.shape, jnp.float32),
            jax.ShapeDtypeStruct(key_all.shape, jnp.float32),
            jax.ShapeDtypeStruct(value_all.shape, jnp.float32),
        ),
        in_specs=[band_spec, head_cols, head_cols, kv_cols, kv_cols],
        out_specs=(head_cols, kv_cols, kv_cols),
    )(band_rel.reshape(tok_rows, 1), queries, out_grad, key_all, value_all)


def shifted(value, axis, steps):
    count = lax.axis_size(axis)
    initial, last = (max(0, -steps), min(count, count - steps))
    return lax.ppermute(value, axis, [(source, source + steps) for source in range(initial, last)])


def rope_tables(positions, head_size):
    half_size = head_size // 2
    frequency = jnp.power(
        rotary_frequency_base, -2.0 * jnp.arange(half_size, dtype=jnp.float32) / head_size
    )
    angles = positions.astype(jnp.float32)[:, None] * frequency[None, :]
    cosine_table = jnp.concatenate([jnp.cos(angles), jnp.cos(angles)], 1)
    sine_table = jnp.concatenate([jnp.sin(angles), jnp.sin(angles)], 1)
    return (cosine_table, sine_table)


def unrotate(gradient, cosine_table, sine_table):
    half_size = gradient.shape[-1] // 2
    scaled = gradient * sine_table
    turned = jnp.concatenate([-scaled[..., half_size:], scaled[..., :half_size]], -1)
    return gradient * cosine_table - turned


def arrange_features(rows, seq_count):
    full_blocks = D // BLOCK
    piece = BLOCK // seq_count
    tail_piece = (D - full_blocks * BLOCK) // seq_count
    count = rows.shape[0]
    main = rows[:, : full_blocks * BLOCK].reshape(count, full_blocks, seq_count, piece)
    main = main.transpose(0, 2, 1, 3).reshape(count, seq_count, full_blocks * piece)
    tail = rows[:, full_blocks * BLOCK :].reshape(count, seq_count, tail_piece)
    return jnp.concatenate([main, tail], 2).reshape(count, D)


def owned_block(mine, owner_row, block_pick, seq_count):
    full_blocks = D // BLOCK
    piece = BLOCK // seq_count
    tail_piece = (D - full_blocks * BLOCK) // seq_count
    columns = mine.shape[1]
    mine = jnp.concatenate(
        [mine, jnp.zeros((NBLK * piece - mine.shape[0], columns), mine.dtype)], 0
    ).reshape(NBLK, piece, columns)
    destinations = jnp.arange(seq_count, dtype=jnp.int32)
    dest_block = jnp.sum(
        jnp.where(
            owner_row[None, :] == destinations[:, None],
            jnp.arange(NBLK, dtype=jnp.int32)[None, :],
            0,
        ),
        1,
    )
    send = jnp.take(mine, dest_block, axis=0, mode="clip")
    received = lax.all_to_all(send, "seq", 0, 0, tiled=False)
    main_block = received.reshape(BLOCK, columns)
    tail_block = jnp.concatenate(
        [
            received[:, :tail_piece].reshape(tail_piece * seq_count, columns),
            jnp.zeros((BLOCK - tail_piece * seq_count, columns), received.dtype),
        ],
        0,
    )
    return jnp.where(block_pick == full_blocks, tail_block, main_block)

def per_device(inputs, queries, key_rows, values, out_grad, band_start, owners):
    tok_rows = queries.shape[0]
    seq_count = lax.axis_size("seq")
    seq_index = lax.axis_index("seq")
    group_index = lax.axis_index("head")
    tokens_all = tok_rows * seq_count
    earlier_keys, earlier_values = shifted((key_rows, values), "seq", 1)
    key_all = jnp.concatenate([earlier_keys, key_rows], 0)
    value_all = jnp.concatenate([earlier_values, values], 0)
    band_rel = band_start - (seq_index * tok_rows - WINDOW)
    grad_query, grad_keys, grad_values = attention_backward(
        band_rel, queries, out_grad, key_all, value_all
    )
    grad_keys = grad_keys.reshape(2 * tok_rows, KV_DEV, HD)
    grad_values = grad_values.reshape(2 * tok_rows, KV_DEV, HD)
    rim_keys, rim_values = (
        shifted(grad_keys[:tok_rows].astype(jnp.bfloat16), "seq", -1).astype(jnp.float32),
        shifted(grad_values[:tok_rows].astype(jnp.bfloat16), "seq", -1).astype(jnp.float32),
    )
    own_keys = grad_keys[tok_rows:] + rim_keys
    own_values = grad_values[tok_rows:] + rim_values
    positions = seq_index * tok_rows + jnp.arange(tok_rows, dtype=jnp.int32)
    cosine_table, sine_table = rope_tables(positions, HD)
    query_pre = unrotate(
        grad_query.reshape(tok_rows, KV_DEV * QPK, HD),
        cosine_table[:, None, :],
        sine_table[:, None, :],
    )
    key_pre = unrotate(own_keys, cosine_table[:, None, :], sine_table[:, None, :])
    column_grads = jnp.concatenate(
        [
            query_pre.reshape(tok_rows, KV_DEV * QPK * HD),
            key_pre.reshape(tok_rows, KV_DEV * HD),
            own_values.reshape(tok_rows, KV_DEV * HD),
        ],
        1,
    ).astype(jnp.bfloat16)
    column_count = column_grads.shape[1]
    core = seq_index % 2
    paired = arrange_features(inputs, seq_count).reshape(inputs.shape[0], seq_count // 2, 2, -1)
    local = jnp.concatenate(
        [
            lax.dynamic_index_in_dim(paired, 1 - core, 2, keepdims=False),
            lax.dynamic_index_in_dim(paired, core, 2, keepdims=False),
        ],
        1,
    ).reshape(inputs.shape[0], D)
    head_count = lax.axis_size("head")
    lane_count = head_count // 2
    partner = lax.ppermute(
        local, "head", [(src, (src + lane_count) % head_count) for src in range(head_count)]
    )
    upper = group_index // lane_count
    pair = jnp.stack([local, partner])
    lanes = [list(range(start, start + lane_count)) for start in (0, lane_count)]
    gathered = lax.all_gather(pair, "head", axis=0, tiled=False, axis_index_groups=lanes)
    gathered = gathered.reshape(-1, D)
    halves = column_grads.reshape(2, lane_count, inputs.shape[0], -1)
    halves = lax.dynamic_slice_in_dim(jnp.concatenate([halves, halves], 0), upper, 2, 0)
    column_grads = halves.transpose(1, 0, 2, 3).reshape(column_grads.shape)
    half = D // 2
    given = lax.dot_general(
        gathered[:, :half], column_grads, (((0,), (0,)), ((), ())),
        preferred_element_type=jnp.float32,
    ).astype(jnp.bfloat16)
    taken = lax.ppermute(given, "seq", [(src, src ^ 1) for src in range(seq_count)])
    kept = lax.dot_general(
        gathered[:, half:], column_grads, (((0,), (0,)), ((), ())),
        preferred_element_type=jnp.float32,
    ).astype(jnp.bfloat16)
    kept, taken = lax.optimization_barrier((kept, taken))
    summed = (kept.astype(jnp.float32) + taken.astype(jnp.float32)).astype(jnp.bfloat16)
    groups = [list(range(parity, seq_count, 2)) for parity in range(2)]
    mine = lax.psum_scatter(
        summed, "seq", scatter_dimension=0, tiled=True, axis_index_groups=groups
    )
    owner_row = lax.dynamic_index_in_dim(owners, group_index, 0, keepdims=False)
    is_mine = owner_row == seq_index
    block_pick = jnp.sum(jnp.where(is_mine, jnp.arange(NBLK, dtype=jnp.int32), 0))
    block_part = owned_block(mine, owner_row, block_pick, seq_count)
    def gram_pair(part_rows):
        left_value = (
            lax.dot_general(
                part_rows, part_rows, (((1,), (1,)), ((), ())), preferred_element_type=jnp.float32
            )
            / tokens_all
        )
        right_value = (
            lax.dot_general(
                part_rows, part_rows, (((0,), (0,)), ((), ())), preferred_element_type=jnp.float32
            )
            / tokens_all
        )
        return (left_value, right_value)

    def nothing(part_rows):
        return (
            jnp.zeros((BLOCK, BLOCK), jnp.float32),
            jnp.zeros((column_count, column_count), jnp.float32),
        )

    left_stat, right_stat = lax.cond(jnp.any(is_mine), gram_pair, nothing, block_part)
    return (left_stat[None, None], right_stat[None, None])


def solution(mesh):
    in_specs = (
        P(("seq", "head"), None),
        P("seq", "head"),
        P("seq", "head"),
        P("seq", "head"),
        P("seq", "head"),
        P("seq"),
        P(),
    )
    out_specs = (P("seq", "head", None, None), P("seq", "head", None, None))
    return jax.shard_map(
        per_device, mesh=mesh, in_specs=in_specs, out_specs=out_specs, check_vma=False
    )
```

```python
import jax
import jax.numpy as jnp
from jax import lax
from jax.sharding import PartitionSpec as P
from jax.experimental import pallas as pl
from jax.experimental.pallas import tpu as pltpu

D = 5376
HD = 128
KV_DEV = 2
QPK = 2
WINDOW = 1024
BLOCK = 1024
NBLK = 6


score_scale = 168.0 ** (-0.5)
rotary_frequency_base = 10000.0
neg_large = -1e30
QBLK = 256


def attention_kernel(band_ref, q_ref, do_ref, k_ref, v_ref, dq_ref, dk_ref, dv_ref):
    tok_rows = q_ref.shape[0]
    span = QBLK + WINDOW
    dk_ref[...] = jnp.zeros(dk_ref.shape, jnp.float32)
    dv_ref[...] = jnp.zeros(dv_ref.shape, jnp.float32)
    def one_block(qb, carry):
        q0 = pl.multiple_of(qb * QBLK, QBLK)
        band = band_ref[pl.ds(q0, QBLK), :]
        band = jnp.concatenate([band, band], 0)
        col = lax.broadcasted_iota(jnp.int32, (QPK * QBLK, span), 1)
        row = lax.broadcasted_iota(jnp.int32, (QPK * QBLK, span), 0) % QBLK
        allowed = (col + q0 >= band) & (col <= row + WINDOW)
        for g in range(1):
            base = 0
            qs = jnp.concatenate(
                [q_ref[pl.ds(q0, QBLK), base + r * HD:base + (r + 1) * HD] for r in range(QPK)], 0)
            dos = jnp.concatenate(
                [do_ref[pl.ds(q0, QBLK), base + r * HD:base + (r + 1) * HD] for r in range(QPK)], 0)
            keys = k_ref[pl.ds(q0, span), g * HD:(g + 1) * HD]
            vals = v_ref[pl.ds(q0, span), g * HD:(g + 1) * HD]
            logits = lax.dot_general(qs, keys, (((1,), (1,)), ((), ())),
                                     preferred_element_type=jnp.float32) * score_scale
            masked = jnp.where(allowed, logits, neg_large)
            top = jnp.max(masked, -1, keepdims=True)
            expo = jnp.where(allowed, jnp.exp(masked - top), 0.0)
            attend = expo / jnp.sum(expo, -1, keepdims=True)
            grad_attend = lax.dot_general(dos, vals, (((1,), (1,)), ((), ())),
                                          preferred_element_type=jnp.float32)
            row_dot = jnp.sum(attend * grad_attend, -1, keepdims=True)
            grad_score = (attend * (grad_attend - row_dot) * score_scale).astype(jnp.bfloat16)
            dqs = jnp.dot(grad_score, keys, preferred_element_type=jnp.float32)
            for r in range(QPK):
                dq_ref[pl.ds(q0, QBLK), base + r * HD:base + (r + 1) * HD] = dqs[r * QBLK:(r + 1) * QBLK]
            dk_ref[pl.ds(q0, span), g * HD:(g + 1) * HD] += lax.dot_general(
                grad_score, qs, (((0,), (0,)), ((), ())), preferred_element_type=jnp.float32)
            dv_ref[pl.ds(q0, span), g * HD:(g + 1) * HD] += lax.dot_general(
                attend.astype(jnp.bfloat16), dos, (((0,), (0,)), ((), ())),
                preferred_element_type=jnp.float32)
        return carry

    lax.fori_loop(0, tok_rows // QBLK, one_block, 0)


def attention_backward(band_rel, queries, out_grad, key_all, value_all):
    tok_rows = queries.shape[0]
    head_cols = pl.BlockSpec((tok_rows, QPK * HD), lambda g: (0, g))
    kv_cols = pl.BlockSpec((2 * tok_rows, HD), lambda g: (0, g))
    band_spec = pl.BlockSpec((tok_rows, 1), lambda g: (0, 0))
    return pl.pallas_call(
        attention_kernel,
        grid=(KV_DEV,),
        out_shape=(
            jax.ShapeDtypeStruct(queries.shape, jnp.float32),
            jax.ShapeDtypeStruct(key_all.shape, jnp.float32),
            jax.ShapeDtypeStruct(value_all.shape, jnp.float32),
        ),
        in_specs=[band_spec, head_cols, head_cols, kv_cols, kv_cols],
        out_specs=(head_cols, kv_cols, kv_cols),
    )(band_rel.reshape(tok_rows, 1), queries, out_grad, key_all, value_all)


def shifted(value, axis, steps):
    count = lax.axis_size(axis)
    initial, last = (max(0, -steps), min(count, count - steps))
    return lax.ppermute(value, axis, [(source, source + steps) for source in range(initial, last)])


def rope_tables(positions, head_size):
    half_size = head_size // 2
    frequency = jnp.power(
        rotary_frequency_base, -2.0 * jnp.arange(half_size, dtype=jnp.float32) / head_size
    )
    angles = positions.astype(jnp.float32)[:, None] * frequency[None, :]
    cosine_table = jnp.concatenate([jnp.cos(angles), jnp.cos(angles)], 1)
    sine_table = jnp.concatenate([jnp.sin(angles), jnp.sin(angles)], 1)
    return (cosine_table, sine_table)


def unrotate(gradient, cosine_table, sine_table):
    half_size = gradient.shape[-1] // 2
    scaled = gradient * sine_table
    turned = jnp.concatenate([-scaled[..., half_size:], scaled[..., :half_size]], -1)
    return gradient * cosine_table - turned


def arrange_features(rows, seq_count):
    full_blocks = D // BLOCK
    piece = BLOCK // seq_count
    tail_piece = (D - full_blocks * BLOCK) // seq_count
    count = rows.shape[0]
    main = rows[:, : full_blocks * BLOCK].reshape(count, full_blocks, seq_count, piece)
    main = main.transpose(0, 2, 1, 3).reshape(count, seq_count, full_blocks * piece)
    tail = rows[:, full_blocks * BLOCK :].reshape(count, seq_count, tail_piece)
    return jnp.concatenate([main, tail], 2).reshape(count, D)


def owned_block(mine, owner_row, block_pick, seq_count):
    full_blocks = D // BLOCK
    piece = BLOCK // seq_count
    tail_piece = (D - full_blocks * BLOCK) // seq_count
    columns = mine.shape[1]
    destinations = jnp.arange(seq_count, dtype=jnp.int32)
    dest_block = jnp.sum(
        jnp.where(
            owner_row[None, :] == destinations[:, None],
            jnp.arange(NBLK, dtype=jnp.int32)[None, :],
            0,
        ),
        1,
    )
    rows = dest_block[:, None] * piece + jnp.arange(piece, dtype=jnp.int32)[None, :]
    send = jnp.take(mine, rows, axis=0, mode="clip")
    received = lax.all_to_all(send, "seq", 0, 0, tiled=False)
    main_block = received.reshape(BLOCK, columns)
    tail_block = jnp.concatenate(
        [
            received[:, :tail_piece].reshape(tail_piece * seq_count, columns),
            jnp.zeros((BLOCK - tail_piece * seq_count, columns), received.dtype),
        ],
        0,
    )
    return jnp.where(block_pick == full_blocks, tail_block, main_block)

def per_device(inputs, queries, key_rows, values, out_grad, band_start, owners):
    tok_rows = queries.shape[0]
    seq_count = lax.axis_size("seq")
    seq_index = lax.axis_index("seq")
    group_index = lax.axis_index("head")
    tokens_all = tok_rows * seq_count
    earlier_keys, earlier_values = shifted((key_rows, values), "seq", 1)
    key_all = jnp.concatenate([earlier_keys, key_rows], 0)
    value_all = jnp.concatenate([earlier_values, values], 0)
    band_rel = band_start - (seq_index * tok_rows - WINDOW)
    grad_query, grad_keys, grad_values = attention_backward(
        band_rel, queries, out_grad, key_all, value_all
    )
    grad_keys = grad_keys.reshape(2 * tok_rows, KV_DEV, HD)
    grad_values = grad_values.reshape(2 * tok_rows, KV_DEV, HD)
    rim_keys, rim_values = (
        shifted(grad_keys[:tok_rows].astype(jnp.bfloat16), "seq", -1).astype(jnp.float32),
        shifted(grad_values[:tok_rows].astype(jnp.bfloat16), "seq", -1).astype(jnp.float32),
    )
    own_keys = grad_keys[tok_rows:] + rim_keys
    own_values = grad_values[tok_rows:] + rim_values
    positions = seq_index * tok_rows + jnp.arange(tok_rows, dtype=jnp.int32)
    cosine_table, sine_table = rope_tables(positions, HD)
    query_pre = unrotate(
        grad_query.reshape(tok_rows, KV_DEV * QPK, HD),
        cosine_table[:, None, :],
        sine_table[:, None, :],
    )
    key_pre = unrotate(own_keys, cosine_table[:, None, :], sine_table[:, None, :])
    column_grads = jnp.concatenate(
        [
            query_pre.reshape(tok_rows, KV_DEV * QPK * HD),
            key_pre.reshape(tok_rows, KV_DEV * HD),
            own_values.reshape(tok_rows, KV_DEV * HD),
        ],
        1,
    ).astype(jnp.bfloat16)
    column_count = column_grads.shape[1]
    core = seq_index % 2
    paired = arrange_features(inputs, seq_count).reshape(inputs.shape[0], seq_count // 2, 2, -1)
    local = jnp.concatenate(
        [
            lax.dynamic_index_in_dim(paired, 1 - core, 2, keepdims=False),
            lax.dynamic_index_in_dim(paired, core, 2, keepdims=False),
        ],
        1,
    ).reshape(inputs.shape[0], D)
    head_count = lax.axis_size("head")
    lane_count = head_count // 2
    partner = lax.ppermute(
        local, "head", [(src, (src + lane_count) % head_count) for src in range(head_count)]
    )
    upper = group_index // lane_count
    pair = jnp.stack([local, partner])
    lanes = [list(range(start, start + lane_count)) for start in (0, lane_count)]
    gathered = lax.all_gather(pair, "head", axis=0, tiled=False, axis_index_groups=lanes)
    gathered = gathered.reshape(-1, D)
    halves = column_grads.reshape(2, lane_count, inputs.shape[0], -1)
    halves = lax.dynamic_slice_in_dim(jnp.concatenate([halves, halves], 0), upper, 2, 0)
    column_grads = halves.transpose(1, 0, 2, 3).reshape(column_grads.shape)
    half = D // 2
    given = lax.dot_general(
        gathered[:, :half], column_grads, (((0,), (0,)), ((), ())),
        preferred_element_type=jnp.float32,
    ).astype(jnp.bfloat16)
    taken = lax.ppermute(given, "seq", [(src, src ^ 1) for src in range(seq_count)])
    kept = lax.dot_general(
        gathered[:, half:], column_grads, (((0,), (0,)), ((), ())),
        preferred_element_type=jnp.float32,
    ).astype(jnp.bfloat16)
    kept, taken = lax.optimization_barrier((kept, taken))
    summed = (kept.astype(jnp.float32) + taken.astype(jnp.float32)).astype(jnp.bfloat16)
    groups = [list(range(parity, seq_count, 2)) for parity in range(2)]
    mine = lax.psum_scatter(
        summed, "seq", scatter_dimension=0, tiled=True, axis_index_groups=groups
    )
    owner_row = lax.dynamic_index_in_dim(owners, group_index, 0, keepdims=False)
    is_mine = owner_row == seq_index
    block_pick = jnp.sum(jnp.where(is_mine, jnp.arange(NBLK, dtype=jnp.int32), 0))
    block_part = owned_block(mine, owner_row, block_pick, seq_count)
    def gram_pair(part_rows):
        left_value = (
            lax.dot_general(
                part_rows, part_rows, (((1,), (1,)), ((), ())), preferred_element_type=jnp.float32
            )
            / tokens_all
        )
        right_value = (
            lax.dot_general(
                part_rows, part_rows, (((0,), (0,)), ((), ())), preferred_element_type=jnp.float32
            )
            / tokens_all
        )
        return (left_value, right_value)

    def nothing(part_rows):
        return (
            jnp.zeros((BLOCK, BLOCK), jnp.float32),
            jnp.zeros((column_count, column_count), jnp.float32),
        )

    left_stat, right_stat = lax.cond(jnp.any(is_mine), gram_pair, nothing, block_part)
    return (left_stat[None, None], right_stat[None, None])


def solution(mesh):
    in_specs = (
        P(("seq", "head"), None),
        P("seq", "head"),
        P("seq", "head"),
        P("seq", "head"),
        P("seq", "head"),
        P("seq"),
        P(),
    )
    out_specs = (P("seq", "head", None, None), P("seq", "head", None, None))
    return jax.shard_map(
        per_device, mesh=mesh, in_specs=in_specs, out_specs=out_specs, check_vma=False
    )
```
